256 devices in a mesh: group: 32 (over x, z_lo, core), tp: 8 (over y, z_hi).
Axes of the slice: x: 4, y: 4, z: 8 (z_hi: 2, z_lo: 4; z = z_hi * 4 + z_lo), core: 2. Of those that a mesh axis runs over, the one named last changes fastest.
Arguments:
- prefill_x: bfloat16 [16384, 4096], P('group', 'tp'), may hold values from -6 to 6
- decode_x: bfloat16 [128, 4096], P('group', 'tp'), may hold values from -6 to 6
- ln_gain: float32 [4096], replicated, may hold values from 0.1 to 1.9
- ln_bias: float32 [4096], replicated, may hold values from -3 to 3
- qkv_weight: bfloat16 [4096, 3, 2048], P(None, None, 'tp'), may hold values from -0.09375 to 0.09375
- qkv_bias: float32 [3, 2048], P(None, 'tp'), may hold values from -3 to 3
- prior_cache: bfloat16 [32, 2, 512, 2048], P('group', None, None, 'tp'), may hold values from -144 to 144, as said below
- prefill_offset: int32 [32], P('group'), may hold values from 0 to 512, as said below
- home_cache: bfloat16 [128, 2, 256, 2048], P('group', None, None, 'tp'), may hold values from -144 to 144, as said below
- piece_len: int32 [128, 3], P('group'), may hold values from 0 to 1024, as said below
- side_store: bfloat16 [256, 2, 1024, 2048], P('group', None, None, 'tp'), may hold values from -144 to 144, as said below
Outputs:
- prefill_out: bfloat16 [16384, 2048], P('group', 'tp')
- decode_out: bfloat16 [128, 2048], P('group', 'tp')
The draws below stay inside these ranges and needn't reach their ends.
Inputs may be any that keep to these rules, and one draw needn't show every extreme that they name: `prior_cache`: keys already rotated. `prefill_offset`: the largest value, 512, and 0 occur in every draw. `home_cache`: keys already rotated. `piece_len`: columns 0 and 2 are at most 1024 and reach it in every draw, 0 meaning no piece on that side; column 1 is 1 to 256 and reaches 256 in every draw. `side_store`: keys already rotated.
All inputs are finite; a program needn't handle non-finite values.
Results may differ from the reference program's by a relative error of at most 0.019.
The reference program's roundings to bfloat16 on the way count: a program that leaves them out, or rounds other values in their place, can miss the bound.
Values may be sent and summed in bfloat16 or wider, within the bound.
No kernel may reach another device: no remote copies, remote signals or barrier semaphores. Data moves between devices by JAX's collectives and lax.ppermute only.
A program may use at most 128 MiB of HBM per device.

```python
import math
from functools import reduce
import jax
import jax.numpy as jnp
from jax import lax

D = 4096
HEADS = 16
HD = 128
ROT = 32
P_SIZE = 512
RQ = 4
LP = 512
LH = 256
LS = 1024
GROUPS = 32
NP = 16384
NR = 128
HH = 2048


def cache_block(key, shape):
    base = jnp.clip(jax.random.normal(key, shape, jnp.float32), -4.0, 4.0)
    scale_shape = shape[:-1] + (1,)
    scales = 3.0 * jnp.ones(scale_shape, jnp.float32)
    which = jnp.arange(2).reshape(2, 1, 1)
    factor = jnp.where(which == 0, scales, 1.0)
    return (base * factor).astype(jnp.bfloat16)


def draw_prior_cache(key, part):
    return cache_block(jax.random.fold_in(key, 1), (GROUPS, 2, LP, HEADS * HD))


def draw_home_cache(key, part):
    return cache_block(jax.random.fold_in(key, 2), (NR, 2, LH, HEADS * HD))


def draw_side_store(key, part):
    return cache_block(jax.random.fold_in(key, 3), (2 * NR, 2, LS, HEADS * HD))


def draw_piece_len(key, part):
    streams = jax.random.split(jax.random.fold_in(key, 4), 6)
    count = NR
    order = jnp.arange(count)
    home = jax.random.randint(streams[0], (count,), 1, LH + 1)
    left = jax.random.randint(streams[1], (count,), (LS + 3) // 4, LS + 1)
    right = jax.random.randint(streams[2], (count,), (LS + 3) // 4, LS + 1)
    left = jnp.where(jax.random.randint(streams[3], (count,), 0, 4) > 0, left, 0)
    right = jnp.where(jax.random.randint(streams[4], (count,), 0, 4) > 0, right, 0)
    picks = jax.random.randint(streams[5], (3,), 0, count)
    home = jnp.where(order == picks[0], LH, home)
    left = jnp.where(order == picks[1], LS, left)
    left = jnp.where(order == (picks[1] + 1) % count, 0, left)
    right = jnp.where(order == picks[2], LS, right)
    return jnp.stack([left, home, right], axis=1).astype(jnp.int32)


def draw_prefill_offset(key, part):
    streams = jax.random.split(jax.random.fold_in(key, 5), 2)
    count = GROUPS
    order = jnp.arange(count)
    offset = jax.random.randint(streams[0], (count,), 0, LP + 1)
    picks = jax.random.randint(streams[1], (1,), 0, count)
    offset = jnp.where(order == picks[0], LP, offset)
    offset = jnp.where(order == (picks[0] + 1) % count, 0, offset)
    return offset.astype(jnp.int32)


def block_scale(rng, dims, cuts, smallest, largest):
    factor_of, own = 1.0, jax.random.fold_in(rng, 6)
    for dim, blocks in cuts:
        heights = jnp.exp(jax.random.uniform(jax.random.fold_in(own, dim), (blocks,), jnp.float32, smallest / len(cuts), largest / len(cuts)))
        factor_of = factor_of * jnp.repeat(heights, dims[dim] // blocks).reshape([-1 if axis == dim else 1 for axis in range(len(dims))])
    return factor_of


def noise(own_key, dims, scale, most, pieces=(), kind=jnp.bfloat16):
    factor_of = block_scale(own_key, dims, pieces, -0.22, 0.18) if pieces else 1.0
    values = jax.random.normal(own_key, dims, jnp.float32) * scale * factor_of
    return jnp.minimum(jnp.maximum(values, -most), most).astype(kind)


def setup_inputs(seed: int = 0) -> dict:
    seeds = jax.random.split(jax.random.key(seed), 12)
    return {
        "prefill_x": noise(seeds[0], (NP, D), 1.0, 6.0, ((0, 32), (1, 8))),
        "decode_x": noise(seeds[1], (NR, D), 1.0, 6.0, ((0, 32), (1, 8))),
        "ln_gain": jnp.clip(1.0 + 0.18 * jax.random.normal(seeds[2], (D,), jnp.float32), 0.1, 1.9),
        "ln_bias": noise(seeds[3], (D,), 0.5, 3.0, (), jnp.float32),
        "qkv_weight": noise(seeds[4], (D, 3, HH), D ** -0.5, 0.09375, ((2, 8),)),
        "qkv_bias": noise(seeds[5], (3, HH), 0.5, 3.0, ((1, 8),), jnp.float32),
        "prior_cache": draw_prior_cache(jax.random.fold_in(seeds[11], 71), 0),
        "prefill_offset": draw_prefill_offset(jax.random.fold_in(seeds[11], 71), 0),
        "home_cache": draw_home_cache(jax.random.fold_in(seeds[11], 71), 0),
        "piece_len": draw_piece_len(jax.random.fold_in(seeds[11], 71), 0),
        "side_store": draw_side_store(jax.random.fold_in(seeds[11], 71), 0),
    }


EPS = 1e-05
NEG = -1e+30

def rounded(values):
    return lax.optimization_barrier(values.astype(jnp.bfloat16)).astype(jnp.float32)

def widen(values):
    return values.astype(jnp.float32)

def layer_norm(rows, gain, shift):
    rows = rows.astype(jnp.float32)
    middle = lax.optimization_barrier(jnp.mean(rows, axis=-1, keepdims=True))
    centred = rows - middle
    spread = lax.optimization_barrier(jnp.mean(centred * centred, axis=-1, keepdims=True))
    return (centred * lax.rsqrt(spread + EPS) * gain + shift).astype(jnp.bfloat16)

def rotate(vectors, positions):
    half = ROT // 2
    steps = jnp.arange(half, dtype=jnp.float32) * (2.0 / ROT)
    frequency = jnp.exp(-math.log(10000.0) * steps)
    angle = positions.astype(jnp.float32)[:, None] * frequency[None, :]
    cosine = jnp.cos(angle)[:, None, :]
    sine = jnp.sin(angle)[:, None, :]
    first = vectors[..., :half]
    second = vectors[..., half:ROT]
    return jnp.concatenate([first * cosine - second * sine, second * cosine + first * sine, vectors[..., ROT:]], axis=-1)

def project(normed, weight, bias, positions):
    count = normed.shape[0]
    width = weight.shape[2]
    mixed = jnp.dot(normed, weight.reshape(weight.shape[0], 3 * width), preferred_element_type=jnp.float32)
    mixed = (mixed + bias.reshape(1, 3 * width)).reshape(count, 3, width // HD, HD)
    query = rotate(mixed[:, 0], positions).astype(jnp.bfloat16)
    fresh_key = rotate(mixed[:, 1], positions).astype(jnp.bfloat16)
    fresh_value = mixed[:, 2].astype(jnp.bfloat16)
    return (query, fresh_key, fresh_value)

def attend_rows(query, keys, values, live):
    scores = jnp.einsum('qhd,khd->hqk', widen(query), widen(keys)) * (1.0 / math.sqrt(HD))
    masked = jnp.where(live[None], scores, NEG)
    highest = lax.optimization_barrier(jnp.max(masked, axis=2, keepdims=True))
    weights = jnp.where(live[None], jnp.exp(masked - highest), 0.0)
    total = lax.optimization_barrier(jnp.sum(weights, axis=2))
    mixed = jnp.einsum('hqk,khd->qhd', rounded(weights), widen(values))
    return (mixed / jnp.transpose(total)[:, :, None]).astype(jnp.bfloat16)

def piece_partial(query, keys, values, live):
    scores = jnp.einsum('hd,khd->hk', widen(query), widen(keys)) * (1.0 / math.sqrt(HD))
    masked = jnp.where(live[None], scores, NEG)
    highest = lax.optimization_barrier(jnp.max(masked, axis=1))
    weights = jnp.where(live[None], jnp.exp(masked - highest[:, None]), 0.0)
    total = lax.optimization_barrier(jnp.sum(weights, axis=1))
    summed = jnp.einsum('hk,khd->hd', rounded(weights), widen(values))
    return (highest, total, summed)

def piece_batch(query, store, lengths):
    count, capacity = (store.shape[0], store.shape[2])
    heads = query.shape[1]
    keys = store[:, 0].reshape(count, capacity, heads, HD)
    values = store[:, 1].reshape(count, capacity, heads, HD)
    live = jnp.arange(capacity)[None, :] < lengths[:, None]
    return jax.vmap(piece_partial)(query, keys, values, live)

def home_partial(query, fresh_key, fresh_value, cache, lengths):
    count, capacity = (cache.shape[0], cache.shape[2])
    heads = query.shape[1]
    keys = jnp.concatenate([cache[:, 0].reshape(count, capacity, heads, HD), fresh_key[:, None]], axis=1)
    values = jnp.concatenate([cache[:, 1].reshape(count, capacity, heads, HD), fresh_value[:, None]], axis=1)
    live = jnp.concatenate([jnp.arange(capacity)[None, :] < lengths[:, None], jnp.ones((count, 1), jnp.bool_)], axis=1)
    return jax.vmap(piece_partial)(query, keys, values, live)

def combine(parts):
    highest = reduce(jnp.maximum, [part[0] for part in parts])
    factors = [jnp.exp(part[0] - highest) for part in parts]
    upper = reduce(jnp.add, [factor[:, :, None] * part[2] for factor, part in zip(factors, parts)])
    lower = reduce(jnp.add, [factor * part[1] for factor, part in zip(factors, parts)])
    return (upper / lower[:, :, None]).astype(jnp.bfloat16)

def reference(prefill_x, decode_x, ln_gain, ln_bias, qkv_weight, qkv_bias, prior_cache, prefill_offset, home_cache, piece_len, side_store):
    prefill_rows = prefill_x.reshape(GROUPS, P_SIZE, D)
    decode_rows = decode_x.reshape(GROUPS, RQ, D)
    home_rows = home_cache.reshape(GROUPS, RQ, 2, LH, HH)
    length_rows = piece_len.reshape(GROUPS, RQ, 3)
    held = side_store.reshape(GROUPS, 2, RQ, 2, LS, HH)

    def one_group(inputs):
        rows, prior, offset, new_rows, cache, lengths, index = inputs
        positions = offset + jnp.arange(P_SIZE, dtype=jnp.int32)
        query, fresh_key, fresh_value = project(layer_norm(rows, ln_gain, ln_bias), qkv_weight, qkv_bias, positions)
        keys = jnp.concatenate([prior[0].reshape(LP, HEADS, HD), fresh_key], axis=0)
        values = jnp.concatenate([prior[1].reshape(LP, HEADS, HD), fresh_value], axis=0)
        live = jnp.concatenate([jnp.broadcast_to(jnp.arange(LP)[None, :] < offset, (P_SIZE, LP)), jnp.arange(P_SIZE)[None, :] <= jnp.arange(P_SIZE)[:, None]], axis=1)
        prefill_part = attend_rows(query, keys, values, live).reshape(P_SIZE, HH)
        places = lengths[:, 0] + lengths[:, 1] + lengths[:, 2]
        new_query, new_key, new_value = project(layer_norm(new_rows, ln_gain, ln_bias), qkv_weight, qkv_bias, places)
        right_piece = lax.dynamic_index_in_dim(held, (index + 1) % GROUPS, 0, keepdims=False)[0]
        left_piece = lax.dynamic_index_in_dim(held, (index + GROUPS - 1) % GROUPS, 0, keepdims=False)[1]
        left_parts = piece_batch(new_query, left_piece, lengths[:, 0])
        home_parts = home_partial(new_query, new_key, new_value, cache, lengths[:, 1])
        right_parts = piece_batch(new_query, right_piece, lengths[:, 2])
        decode_part = combine([left_parts, home_parts, right_parts]).reshape(RQ, HH)
        return (prefill_part, decode_part)
    prefill_out, decode_out = lax.map(one_group, (prefill_rows, prior_cache, prefill_offset, decode_rows, home_rows, length_rows, jnp.arange(GROUPS, dtype=jnp.int32)))
    return (prefill_out.reshape(NP, HH), decode_out.reshape(NR, HH))
```

```python
from functools import reduce
import math

import jax
import jax.numpy as jnp
from jax import lax
from jax.sharding import PartitionSpec as P

HD = 128
ROT = 32


EPS = 1e-05
NEG = -1e30


def with_halo(block, sides, width):
    for axis, dim in sides:
        count = lax.axis_size(axis)
        forward = [(i, i + 1) for i in range(count - 1)]
        forward.append((count - 1, 0))
        backward = [(target, source) for source, target in forward]
        low = lax.ppermute(
            lax.slice_in_dim(block, block.shape[dim] - width, None, axis=dim), axis, forward
        )
        high = lax.ppermute(lax.slice_in_dim(block, 0, width, axis=dim), axis, backward)
        block = jnp.concatenate([low, block, high], axis=dim)
    return block


def layer_norm(rows, gain, shift):
    rows = rows.astype(jnp.float32)
    middle = jnp.mean(rows, axis=-1, keepdims=True)
    centred = rows - middle
    spread = jnp.mean(centred * centred, axis=-1, keepdims=True)
    return (centred * lax.rsqrt(spread + EPS) * gain + shift).astype(jnp.bfloat16)


def rotate(vectors, positions):
    half = ROT // 2
    steps = jnp.arange(half, dtype=jnp.float32) * (2.0 / ROT)
    frequency = jnp.exp(-math.log(10000.0) * steps)
    angle = positions.astype(jnp.float32)[:, None] * frequency[None, :]
    cosine = jnp.cos(angle)[:, None, :]
    sine = jnp.sin(angle)[:, None, :]
    first = vectors[..., :half]
    second = vectors[..., half:ROT]
    return jnp.concatenate(
        [first * cosine - second * sine, second * cosine + first * sine, vectors[..., ROT:]],
        axis=-1,
    )


def project(normed, weight, bias, positions):
    count = normed.shape[0]
    width = weight.shape[2]
    mixed = jnp.dot(
        normed, weight.reshape(weight.shape[0], 3 * width), preferred_element_type=jnp.float32
    )
    mixed = (mixed + bias.reshape(1, 3 * width)).reshape(count, 3, width // HD, HD)
    query = rotate(mixed[:, 0], positions).astype(jnp.bfloat16)
    fresh_key = rotate(mixed[:, 1], positions).astype(jnp.bfloat16)
    fresh_value = mixed[:, 2].astype(jnp.bfloat16)
    return (query, fresh_key, fresh_value)


def attend_rows(query, keys, values, live):
    scores = jnp.einsum("qhd,khd->hqk", query, keys, preferred_element_type=jnp.float32) * (
        1.0 / math.sqrt(HD)
    )
    masked = jnp.where(live[None], scores, NEG)
    highest = jnp.max(masked, axis=2, keepdims=True)
    weights = jnp.where(live[None], jnp.exp(masked - highest), 0.0)
    total = jnp.sum(weights, axis=2)
    mixed = jnp.einsum(
        "hqk,khd->qhd", weights.astype(jnp.bfloat16), values, preferred_element_type=jnp.float32
    )
    return (mixed / jnp.transpose(total)[:, :, None]).astype(jnp.bfloat16)


def prefill_attend(query, fresh_key, fresh_value, prior, offset):
    count, heads = (query.shape[0], query.shape[1])
    capacity = prior.shape[1]
    keys = jnp.concatenate([prior[0].reshape(capacity, heads, HD), fresh_key], axis=0)
    values = jnp.concatenate([prior[1].reshape(capacity, heads, HD), fresh_value], axis=0)
    block = min(count, 512)

    def one_block(start):
        places = start + jnp.arange(block, dtype=jnp.int32)
        live = jnp.concatenate(
            [
                jnp.broadcast_to(jnp.arange(capacity)[None, :] < offset, (block, capacity)),
                jnp.arange(count)[None, :] <= places[:, None],
            ],
            axis=1,
        )
        return attend_rows(query, keys, values, live)

    starts = jnp.arange(count // block, dtype=jnp.int32) * block
    return lax.map(one_block, starts).reshape(count, heads * HD)


def piece_partial(query, keys, values, live):
    scores = jnp.einsum("hd,khd->hk", query, keys, preferred_element_type=jnp.float32) * (
        1.0 / math.sqrt(HD)
    )
    masked = jnp.where(live[None], scores, NEG)
    highest = jnp.max(masked, axis=1)
    weights = jnp.where(live[None], jnp.exp(masked - highest[:, None]), 0.0)
    total = jnp.sum(weights, axis=1)
    summed = jnp.einsum(
        "hk,khd->hd", weights.astype(jnp.bfloat16), values, preferred_element_type=jnp.float32
    )
    return (highest, total, summed)


def piece_batch(query, store, lengths):
    count, capacity = (store.shape[0], store.shape[2])
    heads = query.shape[1]
    keys = store[:, 0].reshape(count, capacity, heads, HD)
    values = store[:, 1].reshape(count, capacity, heads, HD)
    live = jnp.arange(capacity)[None, :] < lengths[:, None]
    return jax.vmap(piece_partial)(query, keys, values, live)


def home_partial(query, fresh_key, fresh_value, cache, lengths):
    count, capacity = (cache.shape[0], cache.shape[2])
    heads = query.shape[1]
    keys = jnp.concatenate(
        [cache[:, 0].reshape(count, capacity, heads, HD), fresh_key[:, None]], axis=1
    )
    values = jnp.concatenate(
        [cache[:, 1].reshape(count, capacity, heads, HD), fresh_value[:, None]], axis=1
    )
    live = jnp.concatenate(
        [jnp.arange(capacity)[None, :] < lengths[:, None], jnp.ones((count, 1), jnp.bool_)], axis=1
    )
    return jax.vmap(piece_partial)(query, keys, values, live)


def combine(parts):
    highest = reduce(jnp.maximum, [part[0] for part in parts])
    factors = [jnp.exp(part[0] - highest) for part in parts]
    upper = reduce(jnp.add, [factor[:, :, None] * part[2] for factor, part in zip(factors, parts)])
    lower = reduce(jnp.add, [factor * part[1] for factor, part in zip(factors, parts)])
    return (upper / lower[:, :, None]).astype(jnp.bfloat16)


def local(
    prefill_x,
    decode_x,
    ln_gain,
    ln_bias,
    qkv_weight,
    qkv_bias,
    prior_cache,
    prefill_offset,
    home_cache,
    piece_len,
    side_store,
):
    count = prefill_x.shape[0]
    requests = decode_x.shape[0]
    whole = lax.all_gather(
        jnp.concatenate([prefill_x, decode_x], axis=0), "tp", axis=1, tiled=True
    )
    normed = layer_norm(whole, ln_gain, ln_bias)
    positions = jnp.concatenate(
        [
            prefill_offset[0] + jnp.arange(count, dtype=jnp.int32),
            piece_len[:, 0] + piece_len[:, 1] + piece_len[:, 2],
        ],
        axis=0,
    )
    query, fresh_key, fresh_value = project(normed, qkv_weight, qkv_bias, positions)
    own_query = query[count:]
    home_parts = home_partial(
        own_query, fresh_key[count:], fresh_value[count:], home_cache, piece_len[:, 1]
    )
    groups = lax.axis_size("group")
    forward = [(i, (i + 1) % groups) for i in range(groups)]
    backward = [((i + 1) % groups, i) for i in range(groups)]
    heads = own_query.shape[1]

    def ask(lengths, pairs):
        packed = jnp.concatenate(
            [own_query.astype(jnp.float32).reshape(requests, -1), lengths[:, None].astype(jnp.float32)],
            axis=1,
        )
        got = lax.ppermute(packed, "group", pairs)
        return got[:, :-1].reshape(own_query.shape).astype(own_query.dtype), got[:, -1].astype(jnp.int32)

    def answer(parts, pairs):
        highest, total, summed = parts
        packed = jnp.concatenate([summed, highest[:, :, None], total[:, :, None]], axis=2)
        got = lax.ppermute(packed, "group", pairs)
        return (got[:, :, HD], got[:, :, HD + 1], got[:, :, :HD])

    prev_query, prev_len = ask(piece_len[:, 2], forward)
    next_query, next_len = ask(piece_len[:, 0], backward)
    right_parts = answer(piece_batch(prev_query, side_store[:requests], prev_len), backward)
    left_parts = answer(piece_batch(next_query, side_store[requests:], next_len), forward)
    prefill_out = prefill_attend(
        query[:count], fresh_key[:count], fresh_value[:count], prior_cache[0], prefill_offset[0]
    )
    decode_out = combine([left_parts, home_parts, right_parts]).reshape(requests, -1)
    return (prefill_out, decode_out)


def solution(mesh):
    return jax.shard_map(
        local,
        mesh=mesh,
        in_specs=(
            P("group", "tp"),
            P("group", "tp"),
            P(),
            P(),
            P(None, None, "tp"),
            P(None, "tp"),
            P("group", None, None, "tp"),
            P("group"),
            P("group", None, None, "tp"),
            P("group", None),
            P("group", None, None, "tp"),
        ),
        out_specs=(P("group", "tp"), P("group", "tp")),
        check_vma=False,
    )
```

```python
from functools import reduce
import math

import jax
import jax.numpy as jnp
from jax import lax
from jax.sharding import PartitionSpec as P

HD = 128
ROT = 32


EPS = 1e-05
NEG = -1e30


def with_halo(block, sides, width):
    for axis, dim in sides:
        count = lax.axis_size(axis)
        forward = [(i, i + 1) for i in range(count - 1)]
        forward.append((count - 1, 0))
        backward = [(target, source) for source, target in forward]
        low = lax.ppermute(
            lax.slice_in_dim(block, block.shape[dim] - width, None, axis=dim), axis, forward
        )
        high = lax.ppermute(lax.slice_in_dim(block, 0, width, axis=dim), axis, backward)
        block = jnp.concatenate([low, block, high], axis=dim)
    return block


def layer_norm(rows, gain, shift):
    rows = rows.astype(jnp.float32)
    middle = jnp.mean(rows, axis=-1, keepdims=True)
    centred = rows - middle
    spread = jnp.mean(centred * centred, axis=-1, keepdims=True)
    return (centred * lax.rsqrt(spread + EPS) * gain + shift).astype(jnp.bfloat16)


def rotate(vectors, positions):
    half = ROT // 2
    steps = jnp.arange(half, dtype=jnp.float32) * (2.0 / ROT)
    frequency = jnp.exp(-math.log(10000.0) * steps)
    angle = positions.astype(jnp.float32)[:, None] * frequency[None, :]
    cosine = jnp.cos(angle)[:, None, :]
    sine = jnp.sin(angle)[:, None, :]
    first = vectors[..., :half]
    second = vectors[..., half:ROT]
    return jnp.concatenate(
        [first * cosine - second * sine, second * cosine + first * sine, vectors[..., ROT:]],
        axis=-1,
    )


def project(normed, weight, bias, positions):
    count = normed.shape[0]
    width = weight.shape[2]
    mixed = jnp.dot(
        normed, weight.reshape(weight.shape[0], 3 * width), preferred_element_type=jnp.float32
    )
    mixed = (mixed + bias.reshape(1, 3 * width)).reshape(count, 3, width // HD, HD)
    query = rotate(mixed[:, 0], positions).astype(jnp.bfloat16)
    fresh_key = rotate(mixed[:, 1], positions).astype(jnp.bfloat16)
    fresh_value = mixed[:, 2].astype(jnp.bfloat16)
    return (query, fresh_key, fresh_value)


def attend_rows(query, keys, values, live):
    scores = jnp.einsum("qhd,khd->hqk", query, keys, preferred_element_type=jnp.float32) * (
        1.0 / math.sqrt(HD)
    )
    masked = jnp.where(live[None], scores, NEG)
    highest = jnp.max(masked, axis=2, keepdims=True)
    weights = jnp.where(live[None], jnp.exp(masked - highest), 0.0)
    total = jnp.sum(weights, axis=2)
    mixed = jnp.einsum(
        "hqk,khd->qhd", weights.astype(jnp.bfloat16), values, preferred_element_type=jnp.float32
    )
    return (mixed / jnp.transpose(total)[:, :, None]).astype(jnp.bfloat16)


def prefill_attend(query, fresh_key, fresh_value, prior, offset):
    count, heads = (query.shape[0], query.shape[1])
    capacity = prior.shape[1]
    keys = jnp.concatenate([prior[0].reshape(capacity, heads, HD), fresh_key], axis=0)
    values = jnp.concatenate([prior[1].reshape(capacity, heads, HD), fresh_value], axis=0)
    block = min(count, 512)

    def one_block(start):
        places = start + jnp.arange(block, dtype=jnp.int32)
        live = jnp.concatenate(
            [
                jnp.broadcast_to(jnp.arange(capacity)[None, :] < offset, (block, capacity)),
                jnp.arange(count)[None, :] <= places[:, None],
            ],
            axis=1,
        )
        return attend_rows(query, keys, values, live)

    starts = jnp.arange(count // block, dtype=jnp.int32) * block
    return lax.map(one_block, starts).reshape(count, heads * HD)


def piece_partial(query, keys, values, live):
    scores = jnp.einsum("hd,khd->hk", query, keys, preferred_element_type=jnp.float32) * (
        1.0 / math.sqrt(HD)
    )
    masked = jnp.where(live[None], scores, NEG)
    highest = jnp.max(masked, axis=1)
    weights = jnp.where(live[None], jnp.exp(masked - highest[:, None]), 0.0)
    total = jnp.sum(weights, axis=1)
    summed = jnp.einsum(
        "hk,khd->hd", weights.astype(jnp.bfloat16), values, preferred_element_type=jnp.float32
    )
    return (highest, total, summed)


def piece_batch(query, store, lengths):
    count, capacity = (store.shape[0], store.shape[2])
    heads = query.shape[1]
    keys = store[:, 0].reshape(count, capacity, heads, HD)
    values = store[:, 1].reshape(count, capacity, heads, HD)
    live = jnp.arange(capacity)[None, :] < lengths[:, None]
    return jax.vmap(piece_partial)(query, keys, values, live)


def home_partial(query, fresh_key, fresh_value, cache, lengths):
    count, capacity = (cache.shape[0], cache.shape[2])
    heads = query.shape[1]
    keys = jnp.concatenate(
        [cache[:, 0].reshape(count, capacity, heads, HD), fresh_key[:, None]], axis=1
    )
    values = jnp.concatenate(
        [cache[:, 1].reshape(count, capacity, heads, HD), fresh_value[:, None]], axis=1
    )
    live = jnp.concatenate(
        [jnp.arange(capacity)[None, :] < lengths[:, None], jnp.ones((count, 1), jnp.bool_)], axis=1
    )
    return jax.vmap(piece_partial)(query, keys, values, live)


def combine(parts):
    highest = reduce(jnp.maximum, [part[0] for part in parts])
    factors = [jnp.exp(part[0] - highest) for part in parts]
    upper = reduce(jnp.add, [factor[:, :, None] * part[2] for factor, part in zip(factors, parts)])
    lower = reduce(jnp.add, [factor * part[1] for factor, part in zip(factors, parts)])
    return (upper / lower[:, :, None]).astype(jnp.bfloat16)


def local(
    prefill_x,
    decode_x,
    ln_gain,
    ln_bias,
    qkv_weight,
    qkv_bias,
    prior_cache,
    prefill_offset,
    home_cache,
    piece_len,
    side_store,
):
    count = prefill_x.shape[0]
    requests = decode_x.shape[0]
    half = lax.all_gather(jnp.concatenate([prefill_x, decode_x], axis=0), "tz", axis=1, tiled=True)
    whole = lax.all_gather(half, "ty", axis=1, tiled=True)
    normed = layer_norm(whole, ln_gain, ln_bias)
    positions = jnp.concatenate(
        [
            prefill_offset[0] + jnp.arange(count, dtype=jnp.int32),
            piece_len[:, 0] + piece_len[:, 1] + piece_len[:, 2],
        ],
        axis=0,
    )
    query, fresh_key, fresh_value = project(normed, qkv_weight, qkv_bias, positions)
    own_query = query[count:]
    home_parts = home_partial(
        own_query, fresh_key[count:], fresh_value[count:], home_cache, piece_len[:, 1]
    )
    groups = lax.axis_size("group")
    forward = [(i, (i + 1) % groups) for i in range(groups)]
    backward = [((i + 1) % groups, i) for i in range(groups)]
    heads = own_query.shape[1]

    def ask(lengths, pairs):
        packed = jnp.concatenate(
            [own_query.astype(jnp.float32).reshape(requests, -1), lengths[:, None].astype(jnp.float32)],
            axis=1,
        )
        got = lax.ppermute(packed, "group", pairs)
        return got[:, :-1].reshape(own_query.shape).astype(own_query.dtype), got[:, -1].astype(jnp.int32)

    def answer(parts, pairs):
        highest, total, summed = parts
        packed = jnp.concatenate([summed, highest[:, :, None], total[:, :, None]], axis=2)
        got = lax.ppermute(packed, "group", pairs)
        return (got[:, :, HD], got[:, :, HD + 1], got[:, :, :HD])

    prev_query, prev_len = ask(piece_len[:, 2], forward)
    next_query, next_len = ask(piece_len[:, 0], backward)
    right_parts = answer(piece_batch(prev_query, side_store[:requests], prev_len), backward)
    left_parts = answer(piece_batch(next_query, side_store[requests:], next_len), forward)
    prefill_out = prefill_attend(
        query[:count], fresh_key[:count], fresh_value[:count], prior_cache[0], prefill_offset[0]
    )
    decode_out = combine([left_parts, home_parts, right_parts]).reshape(requests, -1)
    return (prefill_out, decode_out)


def solution(mesh):
    devices = mesh.devices.reshape(mesh.devices.shape[0], -1, 2)
    split = jax.sharding.Mesh(devices, ("group", "ty", "tz"))
    tp = ("ty", "tz")
    inner = jax.shard_map(
        local,
        mesh=split,
        in_specs=(
            P("group", tp),
            P("group", tp),
            P(),
            P(),
            P(None, None, tp),
            P(None, tp),
            P("group", None, None, tp),
            P("group"),
            P("group", None, None, tp),
            P("group", None),
            P("group", None, None, tp),
        ),
        out_specs=(P("group", tp), P("group", tp)),
        check_vma=False,
    )
    return inner
```

```python
from functools import reduce
import math

import jax
import jax.numpy as jnp
from jax import lax
from jax.sharding import PartitionSpec as P

HD = 128
ROT = 32


EPS = 1e-05
NEG = -1e30


def with_halo(block, sides, width):
    for axis, dim in sides:
        count = lax.axis_size(axis)
        forward = [(i, i + 1) for i in range(count - 1)]
        forward.append((count - 1, 0))
        backward = [(target, source) for source, target in forward]
        low = lax.ppermute(
            lax.slice_in_dim(block, block.shape[dim] - width, None, axis=dim), axis, forward
        )
        high = lax.ppermute(lax.slice_in_dim(block, 0, width, axis=dim), axis, backward)
        block = jnp.concatenate([low, block, high], axis=dim)
    return block


def layer_norm(rows, gain, shift):
    rows = rows.astype(jnp.float32)
    middle = jnp.mean(rows, axis=-1, keepdims=True)
    centred = rows - middle
    spread = jnp.mean(centred * centred, axis=-1, keepdims=True)
    return (centred * lax.rsqrt(spread + EPS) * gain + shift).astype(jnp.bfloat16)


def rotate(vectors, positions):
    half = ROT // 2
    steps = jnp.arange(half, dtype=jnp.float32) * (2.0 / ROT)
    frequency = jnp.exp(-math.log(10000.0) * steps)
    angle = positions.astype(jnp.float32)[:, None] * frequency[None, :]
    cosine = jnp.cos(angle)[:, None, :]
    sine = jnp.sin(angle)[:, None, :]
    first = vectors[..., :half]
    second = vectors[..., half:ROT]
    return jnp.concatenate(
        [first * cosine - second * sine, second * cosine + first * sine, vectors[..., ROT:]],
        axis=-1,
    )


def project(normed, weight, bias, positions):
    count = normed.shape[0]
    width = weight.shape[2]
    mixed = jnp.dot(
        normed, weight.reshape(weight.shape[0], 3 * width), preferred_element_type=jnp.float32
    )
    mixed = (mixed + bias.reshape(1, 3 * width)).reshape(count, 3, width // HD, HD)
    query = rotate(mixed[:, 0], positions).astype(jnp.bfloat16)
    fresh_key = rotate(mixed[:, 1], positions).astype(jnp.bfloat16)
    fresh_value = mixed[:, 2].astype(jnp.bfloat16)
    return (query, fresh_key, fresh_value)


def attend_rows(query, keys, values, live):
    scores = jnp.einsum("qhd,khd->hqk", query, keys, preferred_element_type=jnp.float32) * (
        1.0 / math.sqrt(HD)
    )
    masked = jnp.where(live[None], scores, NEG)
    highest = jnp.max(masked, axis=2, keepdims=True)
    weights = jnp.where(live[None], jnp.exp(masked - highest), 0.0)
    total = jnp.sum(weights, axis=2)
    mixed = jnp.einsum(
        "hqk,khd->qhd", weights.astype(jnp.bfloat16), values, preferred_element_type=jnp.float32
    )
    return (mixed / jnp.transpose(total)[:, :, None]).astype(jnp.bfloat16)


def prefill_attend(query, fresh_key, fresh_value, prior, offset):
    count, heads = (query.shape[0], query.shape[1])
    capacity = prior.shape[1]
    keys = jnp.concatenate([prior[0].reshape(capacity, heads, HD), fresh_key], axis=0)
    values = jnp.concatenate([prior[1].reshape(capacity, heads, HD), fresh_value], axis=0)
    block = min(count, 512)

    def one_block(start):
        places = start + jnp.arange(block, dtype=jnp.int32)
        live = jnp.concatenate(
            [
                jnp.broadcast_to(jnp.arange(capacity)[None, :] < offset, (block, capacity)),
                jnp.arange(count)[None, :] <= places[:, None],
            ],
            axis=1,
        )
        return attend_rows(query, keys, values, live)

    starts = jnp.arange(count // block, dtype=jnp.int32) * block
    return lax.map(one_block, starts).reshape(count, heads * HD)


def piece_partial(query, keys, values, live):
    scores = jnp.einsum("hd,khd->hk", query, keys, preferred_element_type=jnp.float32) * (
        1.0 / math.sqrt(HD)
    )
    masked = jnp.where(live[None], scores, NEG)
    highest = jnp.max(masked, axis=1)
    weights = jnp.where(live[None], jnp.exp(masked - highest[:, None]), 0.0)
    total = jnp.sum(weights, axis=1)
    summed = jnp.einsum(
        "hk,khd->hd", weights.astype(jnp.bfloat16), values, preferred_element_type=jnp.float32
    )
    return (highest, total, summed)


def piece_batch(query, store, lengths):
    count, capacity = (store.shape[0], store.shape[2])
    heads = query.shape[1]
    keys = store[:, 0].reshape(count, capacity, heads, HD)
    values = store[:, 1].reshape(count, capacity, heads, HD)
    live = jnp.arange(capacity)[None, :] < lengths[:, None]
    return jax.vmap(piece_partial)(query, keys, values, live)


def home_partial(query, fresh_key, fresh_value, cache, lengths):
    count, capacity = (cache.shape[0], cache.shape[2])
    heads = query.shape[1]
    keys = jnp.concatenate(
        [cache[:, 0].reshape(count, capacity, heads, HD), fresh_key[:, None]], axis=1
    )
    values = jnp.concatenate(
        [cache[:, 1].reshape(count, capacity, heads, HD), fresh_value[:, None]], axis=1
    )
    live = jnp.concatenate(
        [jnp.arange(capacity)[None, :] < lengths[:, None], jnp.ones((count, 1), jnp.bool_)], axis=1
    )
    return jax.vmap(piece_partial)(query, keys, values, live)


def combine(parts):
    highest = reduce(jnp.maximum, [part[0] for part in parts])
    factors = [jnp.exp(part[0] - highest) for part in parts]
    upper = reduce(jnp.add, [factor[:, :, None] * part[2] for factor, part in zip(factors, parts)])
    lower = reduce(jnp.add, [factor * part[1] for factor, part in zip(factors, parts)])
    return (upper / lower[:, :, None]).astype(jnp.bfloat16)


def local(
    prefill_x,
    decode_x,
    ln_gain,
    ln_bias,
    qkv_weight,
    qkv_bias,
    prior_cache,
    prefill_offset,
    home_cache,
    piece_len,
    side_store,
):
    count = prefill_x.shape[0]
    requests = decode_x.shape[0]
    rows = jnp.concatenate([prefill_x, decode_x], axis=0)
    partner = lax.ppermute(rows, "tz", [(0, 1), (1, 0)])
    own_y = lax.all_gather(rows, "ty", axis=1, tiled=True)
    partner_y = lax.all_gather(partner, "ty", axis=1, tiled=True)
    lower = lax.axis_index("tz") == 0
    first = jnp.where(lower, own_y, partner_y).reshape(rows.shape[0], -1, 1, rows.shape[1])
    second = jnp.where(lower, partner_y, own_y).reshape(rows.shape[0], -1, 1, rows.shape[1])
    whole = jnp.concatenate([first, second], axis=2).reshape(rows.shape[0], -1)
    normed = layer_norm(whole, ln_gain, ln_bias)
    positions = jnp.concatenate(
        [
            prefill_offset[0] + jnp.arange(count, dtype=jnp.int32),
            piece_len[:, 0] + piece_len[:, 1] + piece_len[:, 2],
        ],
        axis=0,
    )
    query, fresh_key, fresh_value = project(normed, qkv_weight, qkv_bias, positions)
    own_query = query[count:]
    home_parts = home_partial(
        own_query, fresh_key[count:], fresh_value[count:], home_cache, piece_len[:, 1]
    )
    groups = lax.axis_size("group")
    forward = [(i, (i + 1) % groups) for i in range(groups)]
    backward = [((i + 1) % groups, i) for i in range(groups)]
    heads = own_query.shape[1]

    def ask(lengths, pairs):
        packed = jnp.concatenate(
            [own_query.astype(jnp.float32).reshape(requests, -1), lengths[:, None].astype(jnp.float32)],
            axis=1,
        )
        got = lax.ppermute(packed, "group", pairs)
        return got[:, :-1].reshape(own_query.shape).astype(own_query.dtype), got[:, -1].astype(jnp.int32)

    def answer(parts, pairs):
        highest, total, summed = parts
        packed = jnp.concatenate([summed, highest[:, :, None], total[:, :, None]], axis=2)
        got = lax.ppermute(packed, "group", pairs)
        return (got[:, :, HD], got[:, :, HD + 1], got[:, :, :HD])

    prev_query, prev_len = ask(piece_len[:, 2], forward)
    next_query, next_len = ask(piece_len[:, 0], backward)
    right_parts = answer(piece_batch(prev_query, side_store[:requests], prev_len), backward)
    left_parts = answer(piece_batch(next_query, side_store[requests:], next_len), forward)
    prefill_out = prefill_attend(
        query[:count], fresh_key[:count], fresh_value[:count], prior_cache[0], prefill_offset[0]
    )
    decode_out = combine([left_parts, home_parts, right_parts]).reshape(requests, -1)
    return (prefill_out, decode_out)


def solution(mesh):
    devices = mesh.devices.reshape(mesh.devices.shape[0], -1, 2)
    split = jax.sharding.Mesh(devices, ("group", "ty", "tz"))
    tp = ("ty", "tz")
    inner = jax.shard_map(
        local,
        mesh=split,
        in_specs=(
            P("group", tp),
            P("group", tp),
            P(),
            P(),
            P(None, None, tp),
            P(None, tp),
            P("group", None, None, tp),
            P("group"),
            P("group", None, None, tp),
            P("group", None),
            P("group", None, None, tp),
        ),
        out_specs=(P("group", tp), P("group", tp)),
        check_vma=False,
    )
    return inner
```

```python
from functools import reduce
import math

import jax
import jax.numpy as jnp
from jax import lax
from jax.sharding import PartitionSpec as P

HD = 128
ROT = 32


EPS = 1e-05
NEG = -1e30


def with_halo(block, sides, width):
    for axis, dim in sides:
        count = lax.axis_size(axis)
        forward = [(i, i + 1) for i in range(count - 1)]
        forward.append((count - 1, 0))
        backward = [(target, source) for source, target in forward]
        low = lax.ppermute(
            lax.slice_in_dim(block, block.shape[dim] - width, None, axis=dim), axis, forward
        )
        high = lax.ppermute(lax.slice_in_dim(block, 0, width, axis=dim), axis, backward)
        block = jnp.concatenate([low, block, high], axis=dim)
    return block


def layer_norm(rows, gain, shift):
    rows = rows.astype(jnp.float32)
    middle = jnp.mean(rows, axis=-1, keepdims=True)
    centred = rows - middle
    spread = jnp.mean(centred * centred, axis=-1, keepdims=True)
    return (centred * lax.rsqrt(spread + EPS) * gain + shift).astype(jnp.bfloat16)


def rotate(vectors, positions):
    half = ROT // 2
    steps = jnp.arange(half, dtype=jnp.float32) * (2.0 / ROT)
    frequency = jnp.exp(-math.log(10000.0) * steps)
    angle = positions.astype(jnp.float32)[:, None] * frequency[None, :]
    cosine = jnp.cos(angle)[:, None, :]
    sine = jnp.sin(angle)[:, None, :]
    first = vectors[..., :half]
    second = vectors[..., half:ROT]
    return jnp.concatenate(
        [first * cosine - second * sine, second * cosine + first * sine, vectors[..., ROT:]],
        axis=-1,
    )


def project(normed, weight, bias, positions):
    count = normed.shape[0]
    width = weight.shape[2]
    mixed = jnp.dot(
        normed, weight.reshape(weight.shape[0], 3 * width), preferred_element_type=jnp.float32
    )
    mixed = (mixed + bias.reshape(1, 3 * width)).reshape(count, 3, width // HD, HD)
    query = rotate(mixed[:, 0], positions).astype(jnp.bfloat16)
    fresh_key = rotate(mixed[:, 1], positions).astype(jnp.bfloat16)
    fresh_value = mixed[:, 2].astype(jnp.bfloat16)
    return (query, fresh_key, fresh_value)


def attend_rows(query, keys, values, live):
    scores = jnp.einsum("qhd,khd->hqk", query, keys, preferred_element_type=jnp.float32) * (
        1.0 / math.sqrt(HD)
    )
    masked = jnp.where(live[None], scores, NEG)
    highest = jnp.max(masked, axis=2, keepdims=True)
    weights = jnp.where(live[None], jnp.exp(masked - highest), 0.0)
    total = jnp.sum(weights, axis=2)
    mixed = jnp.einsum(
        "hqk,khd->qhd", weights.astype(jnp.bfloat16), values, preferred_element_type=jnp.float32
    )
    return (mixed / jnp.transpose(total)[:, :, None]).astype(jnp.bfloat16)


def prefill_attend(query, fresh_key, fresh_value, prior, offset):
    count, heads = (query.shape[0], query.shape[1])
    capacity = prior.shape[1]
    keys = jnp.concatenate([prior[0].reshape(capacity, heads, HD), fresh_key], axis=0)
    values = jnp.concatenate([prior[1].reshape(capacity, heads, HD), fresh_value], axis=0)
    block = min(count, 512)

    def one_block(start):
        places = start + jnp.arange(block, dtype=jnp.int32)
        live = jnp.concatenate(
            [
                jnp.broadcast_to(jnp.arange(capacity)[None, :] < offset, (block, capacity)),
                jnp.arange(count)[None, :] <= places[:, None],
            ],
            axis=1,
        )
        return attend_rows(query, keys, values, live)

    starts = jnp.arange(count // block, dtype=jnp.int32) * block
    return lax.map(one_block, starts).reshape(count, heads * HD)


def piece_rows(query, keys, values, live):
    count, heads = query.shape[0], query.shape[1]
    own = jnp.arange(heads)[:, None] == jnp.arange(heads)[None, :]
    spread = jnp.where(own[None, :, None, :], query[:, :, :, None], jnp.zeros((), query.dtype))
    spread = spread.reshape(count, heads * HD, heads)
    scores = jnp.einsum("rkf,rfh->rhk", keys, spread, preferred_element_type=jnp.float32) * (
        1.0 / math.sqrt(HD)
    )
    masked = jnp.where(live[:, None, :], scores, NEG)
    highest = jnp.max(masked, axis=2)
    weights = jnp.where(live[:, None, :], jnp.exp(masked - highest[:, :, None]), 0.0)
    total = jnp.sum(weights, axis=2)
    mixed = jnp.einsum(
        "rhk,rkf->rhf", weights.astype(jnp.bfloat16), values, preferred_element_type=jnp.float32
    ).reshape(count, heads, heads, HD)
    summed = jnp.sum(jnp.where(own[None, :, :, None], mixed, 0.0), axis=2)
    return (highest, total, summed)


def piece_batch(query, store, lengths):
    capacity = store.shape[2]
    live = jnp.arange(capacity)[None, :] < lengths[:, None]
    return piece_rows(query, store[:, 0], store[:, 1], live)


def home_partial(query, fresh_key, fresh_value, cache, lengths):
    count, capacity = (cache.shape[0], cache.shape[2])
    keys = jnp.concatenate([cache[:, 0], fresh_key.reshape(count, 1, -1)], axis=1)
    values = jnp.concatenate([cache[:, 1], fresh_value.reshape(count, 1, -1)], axis=1)
    live = jnp.concatenate(
        [jnp.arange(capacity)[None, :] < lengths[:, None], jnp.ones((count, 1), jnp.bool_)], axis=1
    )
    return piece_rows(query, keys, values, live)


def combine(parts):
    highest = reduce(jnp.maximum, [part[0] for part in parts])
    factors = [jnp.exp(part[0] - highest) for part in parts]
    upper = reduce(jnp.add, [factor[:, :, None] * part[2] for factor, part in zip(factors, parts)])
    lower = reduce(jnp.add, [factor * part[1] for factor, part in zip(factors, parts)])
    return (upper / lower[:, :, None]).astype(jnp.bfloat16)


def local(
    prefill_x,
    decode_x,
    ln_gain,
    ln_bias,
    qkv_weight,
    qkv_bias,
    prior_cache,
    prefill_offset,
    home_cache,
    piece_len,
    side_store,
):
    count = prefill_x.shape[0]
    requests = decode_x.shape[0]
    rows = jnp.concatenate([prefill_x, decode_x], axis=0)
    partner = lax.ppermute(rows, "tz", [(0, 1), (1, 0)])
    own_y = lax.all_gather(rows, "ty", axis=1, tiled=True)
    partner_y = lax.all_gather(partner, "ty", axis=1, tiled=True)
    whole = jnp.concatenate([own_y, partner_y], axis=1)
    z = lax.axis_index("tz")

    def feature_order(table):
        blocks = table.reshape((-1, 2, rows.shape[1]) + table.shape[1:])
        own = lax.dynamic_index_in_dim(blocks, z, 1, keepdims=False)
        other = lax.dynamic_index_in_dim(blocks, 1 - z, 1, keepdims=False)
        return jnp.concatenate([own, other], axis=0).reshape(table.shape)

    normed = layer_norm(whole, feature_order(ln_gain), feature_order(ln_bias))
    qkv_weight = feature_order(qkv_weight)
    positions = jnp.concatenate(
        [
            prefill_offset[0] + jnp.arange(count, dtype=jnp.int32),
            piece_len[:, 0] + piece_len[:, 1] + piece_len[:, 2],
        ],
        axis=0,
    )
    query, fresh_key, fresh_value = project(normed, qkv_weight, qkv_bias, positions)
    own_query = query[count:]
    home_parts = home_partial(
        own_query, fresh_key[count:], fresh_value[count:], home_cache, piece_len[:, 1]
    )
    groups = lax.axis_size("group")
    forward = [(i, (i + 1) % groups) for i in range(groups)]
    backward = [((i + 1) % groups, i) for i in range(groups)]
    heads = own_query.shape[1]

    def ask(lengths, pairs):
        packed = jnp.concatenate(
            [own_query.astype(jnp.float32).reshape(requests, -1), lengths[:, None].astype(jnp.float32)],
            axis=1,
        )
        got = lax.ppermute(packed, "group", pairs)
        return got[:, :-1].reshape(own_query.shape).astype(own_query.dtype), got[:, -1].astype(jnp.int32)

    def answer(parts, pairs):
        highest, total, summed = parts
        packed = jnp.concatenate([summed, highest[:, :, None], total[:, :, None]], axis=2)
        got = lax.ppermute(packed, "group", pairs)
        return (got[:, :, HD], got[:, :, HD + 1], got[:, :, :HD])

    prev_query, prev_len = ask(piece_len[:, 2], forward)
    next_query, next_len = ask(piece_len[:, 0], backward)
    right_parts = answer(piece_batch(prev_query, side_store[:requests], prev_len), backward)
    left_parts = answer(piece_batch(next_query, side_store[requests:], next_len), forward)
    prefill_out = prefill_attend(
        query[:count], fresh_key[:count], fresh_value[:count], prior_cache[0], prefill_offset[0]
    )
    decode_out = combine([left_parts, home_parts, right_parts]).reshape(requests, -1)
    return (prefill_out, decode_out)


def solution(mesh):
    devices = mesh.devices.reshape(mesh.devices.shape[0], -1, 2)
    split = jax.sharding.Mesh(devices, ("group", "ty", "tz"))
    tp = ("ty", "tz")
    inner = jax.shard_map(
        local,
        mesh=split,
        in_specs=(
            P("group", tp),
            P("group", tp),
            P(),
            P(),
            P(None, None, tp),
            P(None, tp),
            P("group", None, None, tp),
            P("group"),
            P("group", None, None, tp),
            P("group", None),
            P("group", None, None, tp),
        ),
        out_specs=(P("group", tp), P("group", tp)),
        check_vma=False,
    )
    return inner
```

```python
from functools import reduce
import math

import jax
import jax.numpy as jnp
from jax import lax
from jax.experimental import pallas as pl
from jax.experimental.pallas import tpu as pltpu
from jax.sharding import PartitionSpec as P

HD = 128
ROT = 32


EPS = 1e-05
NEG = -1e30


def with_halo(block, sides, width):
    for axis, dim in sides:
        count = lax.axis_size(axis)
        forward = [(i, i + 1) for i in range(count - 1)]
        forward.append((count - 1, 0))
        backward = [(target, source) for source, target in forward]
        low = lax.ppermute(
            lax.slice_in_dim(block, block.shape[dim] - width, None, axis=dim), axis, forward
        )
        high = lax.ppermute(lax.slice_in_dim(block, 0, width, axis=dim), axis, backward)
        block = jnp.concatenate([low, block, high], axis=dim)
    return block


def layer_norm(rows, gain, shift):
    rows = rows.astype(jnp.float32)
    middle = jnp.mean(rows, axis=-1, keepdims=True)
    centred = rows - middle
    spread = jnp.mean(centred * centred, axis=-1, keepdims=True)
    return (centred * lax.rsqrt(spread + EPS) * gain + shift).astype(jnp.bfloat16)


def rotate(vectors, positions):
    half = ROT // 2
    steps = jnp.arange(half, dtype=jnp.float32) * (2.0 / ROT)
    frequency = jnp.exp(-math.log(10000.0) * steps)
    angle = positions.astype(jnp.float32)[:, None] * frequency[None, :]
    cosine = jnp.cos(angle)[:, None, :]
    sine = jnp.sin(angle)[:, None, :]
    first = vectors[..., :half]
    second = vectors[..., half:ROT]
    return jnp.concatenate(
        [first * cosine - second * sine, second * cosine + first * sine, vectors[..., ROT:]],
        axis=-1,
    )


def qkv_kernel(order_ref, x_ref, w_ref, o_ref):
    @pl.when(pl.program_id(0) == 0)
    def _():
        o_ref[...] = jnp.zeros_like(o_ref)

    o_ref[...] += jnp.dot(x_ref[...], w_ref[...], preferred_element_type=jnp.float32)


def qkv_matmul(normed, weight, order):
    rows, depth = normed.shape
    width = weight.shape[1]
    blocks = order.shape[0]
    size = depth // blocks
    return pl.pallas_call(
        qkv_kernel,
        out_shape=jax.ShapeDtypeStruct((rows, width), jnp.float32),
        grid_spec=pltpu.PrefetchScalarGridSpec(
            num_scalar_prefetch=1,
            grid=(blocks,),
            in_specs=[
                pl.BlockSpec((rows, size), lambda j, order: (0, j)),
                pl.BlockSpec((size, width), lambda j, order: (order[j], 0)),
            ],
            out_specs=pl.BlockSpec((rows, width), lambda j, order: (0, 0)),
        ),
        compiler_params=pltpu.CompilerParams(dimension_semantics=("arbitrary",)),
        cost_estimate=pl.CostEstimate(
            flops=2 * rows * depth * width,
            bytes_accessed=2 * rows * depth + 2 * depth * width + 4 * rows * width,
            transcendentals=0,
        ),
    )(order, normed, weight)


def project(normed, weight, bias, positions, order):
    count = normed.shape[0]
    width = weight.shape[2]
    mixed = qkv_matmul(normed, weight.reshape(weight.shape[0], 3 * width), order)
    mixed = (mixed + bias.reshape(1, 3 * width)).reshape(count, 3, width // HD, HD)
    query = rotate(mixed[:, 0], positions).astype(jnp.bfloat16)
    fresh_key = rotate(mixed[:, 1], positions).astype(jnp.bfloat16)
    fresh_value = mixed[:, 2].astype(jnp.bfloat16)
    return (query, fresh_key, fresh_value)


def attend_rows(query, keys, values, live):
    scores = jnp.einsum("qhd,khd->hqk", query, keys, preferred_element_type=jnp.float32) * (
        1.0 / math.sqrt(HD)
    )
    masked = jnp.where(live[None], scores, NEG)
    highest = jnp.max(masked, axis=2, keepdims=True)
    weights = jnp.where(live[None], jnp.exp(masked - highest), 0.0)
    total = jnp.sum(weights, axis=2)
    mixed = jnp.einsum(
        "hqk,khd->qhd", weights.astype(jnp.bfloat16), values, preferred_element_type=jnp.float32
    )
    return (mixed / jnp.transpose(total)[:, :, None]).astype(jnp.bfloat16)


def prefill_attend(query, fresh_key, fresh_value, prior, offset):
    count, heads = (query.shape[0], query.shape[1])
    capacity = prior.shape[1]
    keys = jnp.concatenate([prior[0].reshape(capacity, heads, HD), fresh_key], axis=0)
    values = jnp.concatenate([prior[1].reshape(capacity, heads, HD), fresh_value], axis=0)
    block = min(count, 512)

    def one_block(start):
        places = start + jnp.arange(block, dtype=jnp.int32)
        live = jnp.concatenate(
            [
                jnp.broadcast_to(jnp.arange(capacity)[None, :] < offset, (block, capacity)),
                jnp.arange(count)[None, :] <= places[:, None],
            ],
            axis=1,
        )
        return attend_rows(query, keys, values, live)

    starts = jnp.arange(count // block, dtype=jnp.int32) * block
    return lax.map(one_block, starts).reshape(count, heads * HD)


def piece_rows(query, keys, values, live):
    count, heads = query.shape[0], query.shape[1]
    own = jnp.arange(heads)[:, None] == jnp.arange(heads)[None, :]
    spread = jnp.where(own[None, :, None, :], query[:, :, :, None], jnp.zeros((), query.dtype))
    spread = spread.reshape(count, heads * HD, heads)
    scores = jnp.einsum("rkf,rfh->rhk", keys, spread, preferred_element_type=jnp.float32) * (
        1.0 / math.sqrt(HD)
    )
    masked = jnp.where(live[:, None, :], scores, NEG)
    highest = jnp.max(masked, axis=2)
    weights = jnp.where(live[:, None, :], jnp.exp(masked - highest[:, :, None]), 0.0)
    total = jnp.sum(weights, axis=2)
    mixed = jnp.einsum(
        "rhk,rkf->rhf", weights.astype(jnp.bfloat16), values, preferred_element_type=jnp.float32
    ).reshape(count, heads, heads, HD)
    summed = jnp.sum(jnp.where(own[None, :, :, None], mixed, 0.0), axis=2)
    return (highest, total, summed)


def piece_batch(query, store, lengths):
    capacity = store.shape[2]
    live = jnp.arange(capacity)[None, :] < lengths[:, None]
    return piece_rows(query, store[:, 0], store[:, 1], live)


def home_partial(query, fresh_key, fresh_value, cache, lengths):
    count, capacity = (cache.shape[0], cache.shape[2])
    keys = jnp.concatenate([cache[:, 0], fresh_key.reshape(count, 1, -1)], axis=1)
    values = jnp.concatenate([cache[:, 1], fresh_value.reshape(count, 1, -1)], axis=1)
    live = jnp.concatenate(
        [jnp.arange(capacity)[None, :] < lengths[:, None], jnp.ones((count, 1), jnp.bool_)], axis=1
    )
    return piece_rows(query, keys, values, live)


def combine(parts):
    highest = reduce(jnp.maximum, [part[0] for part in parts])
    factors = [jnp.exp(part[0] - highest) for part in parts]
    upper = reduce(jnp.add, [factor[:, :, None] * part[2] for factor, part in zip(factors, parts)])
    lower = reduce(jnp.add, [factor * part[1] for factor, part in zip(factors, parts)])
    return (upper / lower[:, :, None]).astype(jnp.bfloat16)


def local(
    prefill_x,
    decode_x,
    ln_gain,
    ln_bias,
    qkv_weight,
    qkv_bias,
    prior_cache,
    prefill_offset,
    home_cache,
    piece_len,
    side_store,
):
    count = prefill_x.shape[0]
    requests = decode_x.shape[0]
    rows = jnp.concatenate([prefill_x, decode_x], axis=0)
    ring = lax.axis_size("ty")
    y = lax.axis_index("ty")
    z = lax.axis_index("tz")
    up = [(i, (i + 1) % ring) for i in range(ring)]
    down = [(i, (i - 1) % ring) for i in range(ring)]
    half = rows.shape[0] // 2

    def around(block):
        below = lax.ppermute(block, "ty", up)
        above = lax.ppermute(block, "ty", down)
        across = jnp.concatenate(
            [lax.ppermute(below[:half], "ty", up), lax.ppermute(above[half:], "ty", down)], axis=0
        )
        return [block, below, above, across]

    partner = lax.ppermute(rows, "tz", [(0, 1), (1, 0)])
    pieces = around(rows) + around(partner)
    whole = jnp.concatenate(pieces, axis=1)
    spots = jnp.stack([y, (y + ring - 1) % ring, (y + 1) % ring, (y + 2) % ring])
    order = jnp.concatenate([spots * 2 + z, spots * 2 + (1 - z)]).astype(jnp.int32)

    def feature_order(table):
        return table.reshape(order.shape[0], -1)[order].reshape(table.shape)

    normed = layer_norm(whole, feature_order(ln_gain), feature_order(ln_bias))
    positions = jnp.concatenate(
        [
            prefill_offset[0] + jnp.arange(count, dtype=jnp.int32),
            piece_len[:, 0] + piece_len[:, 1] + piece_len[:, 2],
        ],
        axis=0,
    )
    query, fresh_key, fresh_value = project(normed, qkv_weight, qkv_bias, positions, order)
    own_query = query[count:]
    home_parts = home_partial(
        own_query, fresh_key[count:], fresh_value[count:], home_cache, piece_len[:, 1]
    )
    groups = lax.axis_size("group")
    forward = [(i, (i + 1) % groups) for i in range(groups)]
    backward = [((i + 1) % groups, i) for i in range(groups)]
    heads = own_query.shape[1]

    def ask(lengths, pairs):
        packed = jnp.concatenate(
            [own_query.astype(jnp.float32).reshape(requests, -1), lengths[:, None].astype(jnp.float32)],
            axis=1,
        )
        got = lax.ppermute(packed, "group", pairs)
        return got[:, :-1].reshape(own_query.shape).astype(own_query.dtype), got[:, -1].astype(jnp.int32)

    def answer(parts, pairs):
        highest, total, summed = parts
        packed = jnp.concatenate([summed, highest[:, :, None], total[:, :, None]], axis=2)
        got = lax.ppermute(packed, "group", pairs)
        return (got[:, :, HD], got[:, :, HD + 1], got[:, :, :HD])

    prev_query, prev_len = ask(piece_len[:, 2], forward)
    next_query, next_len = ask(piece_len[:, 0], backward)
    right_parts = answer(piece_batch(prev_query, side_store[:requests], prev_len), backward)
    left_parts = answer(piece_batch(next_query, side_store[requests:], next_len), forward)
    prefill_out = prefill_attend(
        query[:count], fresh_key[:count], fresh_value[:count], prior_cache[0], prefill_offset[0]
    )
    decode_out = combine([left_parts, home_parts, right_parts]).reshape(requests, -1)
    return (prefill_out, decode_out)


def solution(mesh):
    devices = mesh.devices.reshape(mesh.devices.shape[0], -1, 2)
    split = jax.sharding.Mesh(devices, ("group", "ty", "tz"))
    tp = ("ty", "tz")
    inner = jax.shard_map(
        local,
        mesh=split,
        in_specs=(
            P("group", tp),
            P("group", tp),
            P(),
            P(),
            P(None, None, tp),
            P(None, tp),
            P("group", None, None, tp),
            P("group"),
            P("group", None, None, tp),
            P("group", None),
            P("group", None, None, tp),
        ),
        out_specs=(P("group", tp), P("group", tp)),
        check_vma=False,
    )
    return inner
```

```python
from functools import reduce
import math

import jax
import jax.numpy as jnp
from jax import lax
from jax.experimental import pallas as pl
from jax.experimental.pallas import tpu as pltpu
from jax.sharding import PartitionSpec as P

HD = 128
ROT = 32


EPS = 1e-05
NEG = -1e30


def with_halo(block, sides, width):
    for axis, dim in sides:
        count = lax.axis_size(axis)
        forward = [(i, i + 1) for i in range(count - 1)]
        forward.append((count - 1, 0))
        backward = [(target, source) for source, target in forward]
        low = lax.ppermute(
            lax.slice_in_dim(block, block.shape[dim] - width, None, axis=dim), axis, forward
        )
        high = lax.ppermute(lax.slice_in_dim(block, 0, width, axis=dim), axis, backward)
        block = jnp.concatenate([low, block, high], axis=dim)
    return block


def layer_norm(rows, gain, shift):
    rows = rows.astype(jnp.float32)
    middle = jnp.mean(rows, axis=-1, keepdims=True)
    centred = rows - middle
    spread = jnp.mean(centred * centred, axis=-1, keepdims=True)
    return (centred * lax.rsqrt(spread + EPS) * gain + shift).astype(jnp.bfloat16)


def rotate(vectors, positions):
    half = ROT // 2
    steps = jnp.arange(half, dtype=jnp.float32) * (2.0 / ROT)
    frequency = jnp.exp(-math.log(10000.0) * steps)
    angle = positions.astype(jnp.float32)[:, None] * frequency[None, :]
    cosine = jnp.cos(angle)[:, None, :]
    sine = jnp.sin(angle)[:, None, :]
    first = vectors[..., :half]
    second = vectors[..., half:ROT]
    return jnp.concatenate(
        [first * cosine - second * sine, second * cosine + first * sine, vectors[..., ROT:]],
        axis=-1,
    )


def qkv_kernel(order_ref, x_ref, w_ref, o_ref):
    @pl.when(pl.program_id(0) == 0)
    def _():
        o_ref[...] = jnp.zeros_like(o_ref)

    width = w_ref.shape[2]
    for c in range(w_ref.shape[0]):
        o_ref[:, c * width : (c + 1) * width] += jnp.dot(
            x_ref[...], w_ref[c], preferred_element_type=jnp.float32
        )


def qkv_matmul(normed, weight, order):
    rows, depth = normed.shape
    parts, _, width = weight.shape
    blocks = order.shape[0]
    size = depth // blocks
    return pl.pallas_call(
        qkv_kernel,
        out_shape=jax.ShapeDtypeStruct((rows, parts * width), jnp.float32),
        grid_spec=pltpu.PrefetchScalarGridSpec(
            num_scalar_prefetch=1,
            grid=(blocks,),
            in_specs=[
                pl.BlockSpec((rows, size), lambda j, order: (0, j)),
                pl.BlockSpec((parts, size, width), lambda j, order: (0, order[j], 0)),
            ],
            out_specs=pl.BlockSpec((rows, parts * width), lambda j, order: (0, 0)),
        ),
        compiler_params=pltpu.CompilerParams(dimension_semantics=("arbitrary",)),
        cost_estimate=pl.CostEstimate(
            flops=2 * rows * depth * parts * width,
            bytes_accessed=2 * rows * depth + 2 * depth * parts * width + 4 * rows * parts * width,
            transcendentals=0,
        ),
    )(order, normed, weight)


def project(normed, weight, bias, positions, order):
    count = normed.shape[0]
    width = weight.shape[2]
    mixed = qkv_matmul(normed, weight, order)
    mixed = (mixed + bias.reshape(1, 3 * width)).reshape(count, 3, width // HD, HD)
    query = rotate(mixed[:, 0], positions).astype(jnp.bfloat16)
    fresh_key = rotate(mixed[:, 1], positions).astype(jnp.bfloat16)
    fresh_value = mixed[:, 2].astype(jnp.bfloat16)
    return (query, fresh_key, fresh_value)


def attend_rows(query, keys, values, live):
    scores = jnp.einsum("qhd,khd->hqk", query, keys, preferred_element_type=jnp.float32) * (
        1.0 / math.sqrt(HD)
    )
    masked = jnp.where(live[None], scores, NEG)
    highest = jnp.max(masked, axis=2, keepdims=True)
    weights = jnp.where(live[None], jnp.exp(masked - highest), 0.0)
    total = jnp.sum(weights, axis=2)
    mixed = jnp.einsum(
        "hqk,khd->qhd", weights.astype(jnp.bfloat16), values, preferred_element_type=jnp.float32
    )
    return (mixed / jnp.transpose(total)[:, :, None]).astype(jnp.bfloat16)


def prefill_attend(query, fresh_key, fresh_value, prior, offset):
    count, heads = (query.shape[0], query.shape[1])
    capacity = prior.shape[1]
    keys = jnp.concatenate([prior[0].reshape(capacity, heads, HD), fresh_key], axis=0)
    values = jnp.concatenate([prior[1].reshape(capacity, heads, HD), fresh_value], axis=0)
    block = min(count, 512)

    def one_block(start):
        places = start + jnp.arange(block, dtype=jnp.int32)
        live = jnp.concatenate(
            [
                jnp.broadcast_to(jnp.arange(capacity)[None, :] < offset, (block, capacity)),
                jnp.arange(count)[None, :] <= places[:, None],
            ],
            axis=1,
        )
        return attend_rows(query, keys, values, live)

    starts = jnp.arange(count // block, dtype=jnp.int32) * block
    return lax.map(one_block, starts).reshape(count, heads * HD)


def piece_rows(query, keys, values, live):
    count, heads = query.shape[0], query.shape[1]
    own = jnp.arange(heads)[:, None] == jnp.arange(heads)[None, :]
    spread = jnp.where(own[None, :, None, :], query[:, :, :, None], jnp.zeros((), query.dtype))
    spread = spread.reshape(count, heads * HD, heads)
    scores = jnp.einsum("rkf,rfh->rhk", keys, spread, preferred_element_type=jnp.float32) * (
        1.0 / math.sqrt(HD)
    )
    masked = jnp.where(live[:, None, :], scores, NEG)
    highest = jnp.max(masked, axis=2)
    weights = jnp.where(live[:, None, :], jnp.exp(masked - highest[:, :, None]), 0.0)
    total = jnp.sum(weights, axis=2)
    mixed = jnp.einsum(
        "rhk,rkf->rhf", weights.astype(jnp.bfloat16), values, preferred_element_type=jnp.float32
    ).reshape(count, heads, heads, HD)
    summed = jnp.sum(jnp.where(own[None, :, :, None], mixed, 0.0), axis=2)
    return (highest, total, summed)


def piece_batch(query, store, lengths):
    capacity = store.shape[2]
    live = jnp.arange(capacity)[None, :] < lengths[:, None]
    return piece_rows(query, store[:, 0], store[:, 1], live)


def home_partial(query, fresh_key, fresh_value, cache, lengths):
    count, capacity = (cache.shape[0], cache.shape[2])
    keys = jnp.concatenate([cache[:, 0], fresh_key.reshape(count, 1, -1)], axis=1)
    values = jnp.concatenate([cache[:, 1], fresh_value.reshape(count, 1, -1)], axis=1)
    live = jnp.concatenate(
        [jnp.arange(capacity)[None, :] < lengths[:, None], jnp.ones((count, 1), jnp.bool_)], axis=1
    )
    return piece_rows(query, keys, values, live)


def combine(parts):
    highest = reduce(jnp.maximum, [part[0] for part in parts])
    factors = [jnp.exp(part[0] - highest) for part in parts]
    upper = reduce(jnp.add, [factor[:, :, None] * part[2] for factor, part in zip(factors, parts)])
    lower = reduce(jnp.add, [factor * part[1] for factor, part in zip(factors, parts)])
    return (upper / lower[:, :, None]).astype(jnp.bfloat16)


def local(
    prefill_x,
    decode_x,
    ln_gain,
    ln_bias,
    qkv_weight,
    qkv_bias,
    prior_cache,
    prefill_offset,
    home_cache,
    piece_len,
    side_store,
):
    count = prefill_x.shape[0]
    requests = decode_x.shape[0]
    rows = jnp.concatenate([prefill_x, decode_x], axis=0)
    ring = lax.axis_size("ty")
    y = lax.axis_index("ty")
    z = lax.axis_index("tz")
    up = [(i, (i + 1) % ring) for i in range(ring)]
    down = [(i, (i - 1) % ring) for i in range(ring)]
    half = rows.shape[0] // 2

    def around(block):
        below = lax.ppermute(block, "ty", up)
        above = lax.ppermute(block, "ty", down)
        across = jnp.concatenate(
            [lax.ppermute(below[:half], "ty", up), lax.ppermute(above[half:], "ty", down)], axis=0
        )
        return [block, below, above, across]

    partner = lax.ppermute(rows, "tz", [(0, 1), (1, 0)])
    pieces = around(rows) + around(partner)
    whole = jnp.concatenate(pieces, axis=1)
    spots = jnp.stack([y, (y + ring - 1) % ring, (y + 1) % ring, (y + 2) % ring])
    order = jnp.concatenate([spots * 2 + z, spots * 2 + (1 - z)]).astype(jnp.int32)

    def feature_order(table):
        return table.reshape(order.shape[0], -1)[order].reshape(table.shape)

    gain, shift = feature_order(ln_gain), feature_order(ln_bias)
    weight = jnp.transpose(qkv_weight, (1, 0, 2))
    own_query, new_key, new_value = project(
        layer_norm(whole[count:], gain, shift),
        weight,
        qkv_bias,
        piece_len[:, 0] + piece_len[:, 1] + piece_len[:, 2],
        order,
    )
    home_parts = home_partial(own_query, new_key, new_value, home_cache, piece_len[:, 1])
    groups = lax.axis_size("group")
    forward = [(i, (i + 1) % groups) for i in range(groups)]
    backward = [((i + 1) % groups, i) for i in range(groups)]
    heads = own_query.shape[1]

    def ask(lengths, pairs):
        packed = jnp.concatenate(
            [own_query.astype(jnp.float32).reshape(requests, -1), lengths[:, None].astype(jnp.float32)],
            axis=1,
        )
        got = lax.ppermute(packed, "group", pairs)
        return got[:, :-1].reshape(own_query.shape).astype(own_query.dtype), got[:, -1].astype(jnp.int32)

    def answer(parts, pairs):
        highest, total, summed = parts
        packed = jnp.concatenate([summed, highest[:, :, None], total[:, :, None]], axis=2)
        got = lax.ppermute(packed, "group", pairs)
        return (got[:, :, HD], got[:, :, HD + 1], got[:, :, :HD])

    prev_query, prev_len = ask(piece_len[:, 2], forward)
    next_query, next_len = ask(piece_len[:, 0], backward)
    right_parts = answer(piece_batch(prev_query, side_store[:requests], prev_len), backward)
    left_parts = answer(piece_batch(next_query, side_store[requests:], next_len), forward)
    query, fresh_key, fresh_value = project(
        layer_norm(whole[:count], gain, shift),
        weight,
        qkv_bias,
        prefill_offset[0] + jnp.arange(count, dtype=jnp.int32),
        order,
    )
    prefill_out = prefill_attend(query, fresh_key, fresh_value, prior_cache[0], prefill_offset[0])
    decode_out = combine([left_parts, home_parts, right_parts]).reshape(requests, -1)
    return (prefill_out, decode_out)


def solution(mesh):
    devices = mesh.devices.reshape(mesh.devices.shape[0], -1, 2)
    split = jax.sharding.Mesh(devices, ("group", "ty", "tz"))
    tp = ("ty", "tz")
    inner = jax.shard_map(
        local,
        mesh=split,
        in_specs=(
            P("group", tp),
            P("group", tp),
            P(),
            P(),
            P(None, None, tp),
            P(None, tp),
            P("group", None, None, tp),
            P("group"),
            P("group", None, None, tp),
            P("group", None),
            P("group", None, None, tp),
        ),
        out_specs=(P("group", tp), P("group", tp)),
        check_vma=False,
    )
    return inner
```

```python
from functools import reduce
import math

import jax
import jax.numpy as jnp
from jax import lax
from jax.experimental import pallas as pl
from jax.experimental.pallas import tpu as pltpu
from jax.sharding import PartitionSpec as P

HD = 128
ROT = 32


EPS = 1e-05
NEG = -1e30


def with_halo(block, sides, width):
    for axis, dim in sides:
        count = lax.axis_size(axis)
        forward = [(i, i + 1) for i in range(count - 1)]
        forward.append((count - 1, 0))
        backward = [(target, source) for source, target in forward]
        low = lax.ppermute(
            lax.slice_in_dim(block, block.shape[dim] - width, None, axis=dim), axis, forward
        )
        high = lax.ppermute(lax.slice_in_dim(block, 0, width, axis=dim), axis, backward)
        block = jnp.concatenate([low, block, high], axis=dim)
    return block


def layer_norm(rows, gain, shift):
    rows = rows.astype(jnp.float32)
    middle = jnp.mean(rows, axis=-1, keepdims=True)
    centred = rows - middle
    spread = jnp.mean(centred * centred, axis=-1, keepdims=True)
    return (centred * lax.rsqrt(spread + EPS) * gain + shift).astype(jnp.bfloat16)


def rotate(vectors, positions):
    half = ROT // 2
    steps = jnp.arange(half, dtype=jnp.float32) * (2.0 / ROT)
    frequency = jnp.exp(-math.log(10000.0) * steps)
    angle = positions.astype(jnp.float32)[:, None] * frequency[None, :]
    cosine = jnp.cos(angle)[:, None, :]
    sine = jnp.sin(angle)[:, None, :]
    first = vectors[..., :half]
    second = vectors[..., half:ROT]
    return jnp.concatenate(
        [first * cosine - second * sine, second * cosine + first * sine, vectors[..., ROT:]],
        axis=-1,
    )


def qkv_kernel(order_ref, x_ref, w_ref, o_ref):
    @pl.when(pl.program_id(0) == 0)
    def _():
        o_ref[...] = jnp.zeros_like(o_ref)

    width = w_ref.shape[2]
    for c in range(w_ref.shape[0]):
        o_ref[:, c * width : (c + 1) * width] += jnp.dot(
            x_ref[...], w_ref[c], preferred_element_type=jnp.float32
        )


def qkv_matmul(normed, weight, order):
    rows, depth = normed.shape
    parts, _, width = weight.shape
    blocks = order.shape[0]
    size = depth // blocks
    return pl.pallas_call(
        qkv_kernel,
        out_shape=jax.ShapeDtypeStruct((rows, parts * width), jnp.float32),
        grid_spec=pltpu.PrefetchScalarGridSpec(
            num_scalar_prefetch=1,
            grid=(blocks,),
            in_specs=[
                pl.BlockSpec((rows, size), lambda j, order: (0, j)),
                pl.BlockSpec((parts, size, width), lambda j, order: (0, order[j], 0)),
            ],
            out_specs=pl.BlockSpec((rows, parts * width), lambda j, order: (0, 0)),
        ),
        compiler_params=pltpu.CompilerParams(dimension_semantics=("arbitrary",)),
        cost_estimate=pl.CostEstimate(
            flops=2 * rows * depth * parts * width,
            bytes_accessed=2 * rows * depth + 2 * depth * parts * width + 4 * rows * parts * width,
            transcendentals=0,
        ),
    )(order, normed, weight)


def project(normed, weight, bias, positions, order):
    count = normed.shape[0]
    width = weight.shape[2]
    mixed = qkv_matmul(normed, weight, order)
    mixed = (mixed + bias.reshape(1, 3 * width)).reshape(count, 3, width // HD, HD)
    query = rotate(mixed[:, 0], positions).astype(jnp.bfloat16)
    fresh_key = rotate(mixed[:, 1], positions).astype(jnp.bfloat16)
    fresh_value = mixed[:, 2].astype(jnp.bfloat16)
    return (query, fresh_key, fresh_value)


def attend_rows(query, keys, values, live):
    scores = jnp.einsum("qhd,khd->hqk", query, keys, preferred_element_type=jnp.float32) * (
        1.0 / math.sqrt(HD)
    )
    masked = jnp.where(live[None], scores, NEG)
    highest = jnp.max(masked, axis=2, keepdims=True)
    weights = jnp.where(live[None], jnp.exp(masked - highest), 0.0)
    total = jnp.sum(weights, axis=2)
    mixed = jnp.einsum(
        "hqk,khd->qhd", weights.astype(jnp.bfloat16), values, preferred_element_type=jnp.float32
    )
    return (mixed / jnp.transpose(total)[:, :, None]).astype(jnp.bfloat16)


def prefill_attend(query, fresh_key, fresh_value, prior, offset):
    count, heads = (query.shape[0], query.shape[1])
    capacity = prior.shape[1]
    keys = jnp.concatenate([prior[0].reshape(capacity, heads, HD), fresh_key], axis=0)
    values = jnp.concatenate([prior[1].reshape(capacity, heads, HD), fresh_value], axis=0)
    block = min(count, 512)

    def one_block(start):
        places = start + jnp.arange(block, dtype=jnp.int32)
        live = jnp.concatenate(
            [
                jnp.broadcast_to(jnp.arange(capacity)[None, :] < offset, (block, capacity)),
                jnp.arange(count)[None, :] <= places[:, None],
            ],
            axis=1,
        )
        return attend_rows(query, keys, values, live)

    starts = jnp.arange(count // block, dtype=jnp.int32) * block
    return lax.map(one_block, starts).reshape(count, heads * HD)


def piece_rows(query, keys, values, live):
    count, heads = query.shape[0], query.shape[1]
    own = jnp.arange(heads)[:, None] == jnp.arange(heads)[None, :]
    spread = jnp.where(own[None, :, None, :], query[:, :, :, None], jnp.zeros((), query.dtype))
    spread = spread.reshape(count, heads * HD, heads)
    scores = jnp.einsum("rkf,rfh->rhk", keys, spread, preferred_element_type=jnp.float32) * (
        1.0 / math.sqrt(HD)
    )
    masked = jnp.where(live[:, None, :], scores, NEG)
    highest = jnp.max(masked, axis=2)
    weights = jnp.where(live[:, None, :], jnp.exp(masked - highest[:, :, None]), 0.0)
    total = jnp.sum(weights, axis=2)
    mixed = jnp.einsum(
        "rhk,rkf->rhf", weights.astype(jnp.bfloat16), values, preferred_element_type=jnp.float32
    ).reshape(count, heads, heads, HD)
    summed = jnp.sum(jnp.where(own[None, :, :, None], mixed, 0.0), axis=2)
    return (highest, total, summed)


def piece_batch(query, store, lengths):
    capacity = store.shape[2]
    live = jnp.arange(capacity)[None, :] < lengths[:, None]
    return piece_rows(query, store[:, 0], store[:, 1], live)


def home_partial(query, fresh_key, fresh_value, cache, lengths):
    count, capacity = (cache.shape[0], cache.shape[2])
    keys = jnp.concatenate([cache[:, 0], fresh_key.reshape(count, 1, -1)], axis=1)
    values = jnp.concatenate([cache[:, 1], fresh_value.reshape(count, 1, -1)], axis=1)
    live = jnp.concatenate(
        [jnp.arange(capacity)[None, :] < lengths[:, None], jnp.ones((count, 1), jnp.bool_)], axis=1
    )
    return piece_rows(query, keys, values, live)


def combine(parts):
    highest = reduce(jnp.maximum, [part[0] for part in parts])
    factors = [jnp.exp(part[0] - highest) for part in parts]
    upper = reduce(jnp.add, [factor[:, :, None] * part[2] for factor, part in zip(factors, parts)])
    lower = reduce(jnp.add, [factor * part[1] for factor, part in zip(factors, parts)])
    return (upper / lower[:, :, None]).astype(jnp.bfloat16)


def local(
    prefill_x,
    decode_x,
    ln_gain,
    ln_bias,
    qkv_weight,
    qkv_bias,
    prior_cache,
    prefill_offset,
    home_cache,
    piece_len,
    side_store,
):
    count = prefill_x.shape[0]
    requests = decode_x.shape[0]
    rows = jnp.concatenate([prefill_x, decode_x], axis=0)
    ring = lax.axis_size("ty")
    y = lax.axis_index("ty")
    z = lax.axis_index("tz")
    up = [(i, (i + 1) % ring) for i in range(ring)]
    down = [(i, (i - 1) % ring) for i in range(ring)]
    half = rows.shape[0] // 2

    def around(block):
        below = lax.ppermute(block, "ty", up)
        above = lax.ppermute(block, "ty", down)
        across = jnp.concatenate(
            [lax.ppermute(below[:half], "ty", up), lax.ppermute(above[half:], "ty", down)], axis=0
        )
        return [block, below, above, across]

    partner = lax.ppermute(rows, "tz", [(0, 1), (1, 0)])
    pieces = around(rows) + around(partner)
    whole = jnp.concatenate(pieces, axis=1)
    spots = jnp.stack([y, (y + ring - 1) % ring, (y + 1) % ring, (y + 2) % ring])
    order = jnp.concatenate([spots * 2 + z, spots * 2 + (1 - z)]).astype(jnp.int32)

    def feature_order(table):
        return table.reshape(order.shape[0], -1)[order].reshape(table.shape)

    gain, shift = feature_order(ln_gain), feature_order(ln_bias)
    weight = jnp.transpose(qkv_weight, (1, 0, 2))
    own_query, new_key, new_value = project(
        layer_norm(whole[count:], gain, shift),
        weight,
        qkv_bias,
        piece_len[:, 0] + piece_len[:, 1] + piece_len[:, 2],
        order,
    )
    home_parts = home_partial(own_query, new_key, new_value, home_cache, piece_len[:, 1])
    groups = lax.axis_size("group")
    forward = [(i, (i + 1) % groups) for i in range(groups)]
    backward = [((i + 1) % groups, i) for i in range(groups)]
    heads = own_query.shape[1]

    def ask(lengths, pairs):
        packed = jnp.concatenate(
            [own_query.astype(jnp.float32).reshape(requests, -1), lengths[:, None].astype(jnp.float32)],
            axis=1,
        )
        got = lax.ppermute(packed, "group", pairs)
        return got[:, :-1].reshape(own_query.shape).astype(own_query.dtype), got[:, -1].astype(jnp.int32)

    def answer(parts, pairs):
        highest, total, summed = parts
        packed = jnp.concatenate([summed, highest[:, :, None], total[:, :, None]], axis=2)
        got = lax.ppermute(packed, "group", pairs)
        return (got[:, :, HD], got[:, :, HD + 1], got[:, :, :HD])

    prev_query, prev_len = ask(piece_len[:, 2], forward)
    next_query, next_len = ask(piece_len[:, 0], backward)
    normed = layer_norm(whole[:count], gain, shift)
    right_for_prev = piece_batch(prev_query, side_store[:requests], prev_len)
    left_for_next = piece_batch(next_query, side_store[requests:], next_len)
    right_for_prev, left_for_next, normed = lax.optimization_barrier(
        (right_for_prev, left_for_next, normed)
    )
    right_parts = answer(right_for_prev, backward)
    left_parts = answer(left_for_next, forward)
    query, fresh_key, fresh_value = project(
        normed,
        weight,
        qkv_bias,
        prefill_offset[0] + jnp.arange(count, dtype=jnp.int32),
        order,
    )
    prefill_out = prefill_attend(query, fresh_key, fresh_value, prior_cache[0], prefill_offset[0])
    decode_out = combine([left_parts, home_parts, right_parts]).reshape(requests, -1)
    return (prefill_out, decode_out)


def solution(mesh):
    devices = mesh.devices.reshape(mesh.devices.shape[0], -1, 2)
    split = jax.sharding.Mesh(devices, ("group", "ty", "tz"))
    tp = ("ty", "tz")
    inner = jax.shard_map(
        local,
        mesh=split,
        in_specs=(
            P("group", tp),
            P("group", tp),
            P(),
            P(),
            P(None, None, tp),
            P(None, tp),
            P("group", None, None, tp),
            P("group"),
            P("group", None, None, tp),
            P("group", None),
            P("group", None, None, tp),
        ),
        out_specs=(P("group", tp), P("group", tp)),
        check_vma=False,
    )
    return inner
```

```python
from functools import reduce
import math

import jax
import jax.numpy as jnp
from jax import lax
from jax.experimental import pallas as pl
from jax.experimental.pallas import tpu as pltpu
from jax.sharding import PartitionSpec as P

HD = 128
ROT = 32


EPS = 1e-05
NEG = -1e30


def with_halo(block, sides, width):
    for axis, dim in sides:
        count = lax.axis_size(axis)
        forward = [(i, i + 1) for i in range(count - 1)]
        forward.append((count - 1, 0))
        backward = [(target, source) for source, target in forward]
        low = lax.ppermute(
            lax.slice_in_dim(block, block.shape[dim] - width, None, axis=dim), axis, forward
        )
        high = lax.ppermute(lax.slice_in_dim(block, 0, width, axis=dim), axis, backward)
        block = jnp.concatenate([low, block, high], axis=dim)
    return block


def layer_norm(rows, gain, shift):
    rows = rows.astype(jnp.float32)
    middle = jnp.mean(rows, axis=-1, keepdims=True)
    centred = rows - middle
    spread = jnp.mean(centred * centred, axis=-1, keepdims=True)
    return (centred * lax.rsqrt(spread + EPS) * gain + shift).astype(jnp.bfloat16)


def rotate(vectors, positions):
    half = ROT // 2
    steps = jnp.arange(half, dtype=jnp.float32) * (2.0 / ROT)
    frequency = jnp.exp(-math.log(10000.0) * steps)
    angle = positions.astype(jnp.float32)[:, None] * frequency[None, :]
    cosine = jnp.cos(angle)[:, None, :]
    sine = jnp.sin(angle)[:, None, :]
    first = vectors[..., :half]
    second = vectors[..., half:ROT]
    return jnp.concatenate(
        [first * cosine - second * sine, second * cosine + first * sine, vectors[..., ROT:]],
        axis=-1,
    )


def qkv_kernel(order_ref, x_ref, w_ref, o_ref):
    @pl.when(pl.program_id(0) == 0)
    def _():
        o_ref[...] = jnp.zeros_like(o_ref)

    width = w_ref.shape[2]
    for c in range(w_ref.shape[0]):
        o_ref[:, c * width : (c + 1) * width] += jnp.dot(
            x_ref[...], w_ref[c], preferred_element_type=jnp.float32
        )


def qkv_matmul(normed, weight, order):
    rows, depth = normed.shape
    parts, _, width = weight.shape
    blocks = order.shape[0]
    size = depth // blocks
    return pl.pallas_call(
        qkv_kernel,
        out_shape=jax.ShapeDtypeStruct((rows, parts * width), jnp.float32),
        grid_spec=pltpu.PrefetchScalarGridSpec(
            num_scalar_prefetch=1,
            grid=(blocks,),
            in_specs=[
                pl.BlockSpec((rows, size), lambda j, order: (0, j)),
                pl.BlockSpec((parts, size, width), lambda j, order: (0, order[j], 0)),
            ],
            out_specs=pl.BlockSpec((rows, parts * width), lambda j, order: (0, 0)),
        ),
        compiler_params=pltpu.CompilerParams(dimension_semantics=("arbitrary",)),
        cost_estimate=pl.CostEstimate(
            flops=2 * rows * depth * parts * width,
            bytes_accessed=2 * rows * depth + 2 * depth * parts * width + 4 * rows * parts * width,
            transcendentals=0,
        ),
    )(order, normed, weight)


def project(normed, weight, bias, positions, order):
    count = normed.shape[0]
    width = weight.shape[2]
    mixed = qkv_matmul(normed, weight, order)
    mixed = (mixed + bias.reshape(1, 3 * width)).reshape(count, 3, width // HD, HD)
    query = rotate(mixed[:, 0], positions).astype(jnp.bfloat16)
    fresh_key = rotate(mixed[:, 1], positions).astype(jnp.bfloat16)
    fresh_value = mixed[:, 2].astype(jnp.bfloat16)
    return (query, fresh_key, fresh_value)


def attend_rows(query, keys, values, live):
    scores = jnp.einsum("qhd,khd->hqk", query, keys, preferred_element_type=jnp.float32) * (
        1.0 / math.sqrt(HD)
    )
    masked = jnp.where(live[None], scores, NEG)
    highest = jnp.max(masked, axis=2, keepdims=True)
    weights = jnp.where(live[None], jnp.exp(masked - highest), 0.0)
    total = jnp.sum(weights, axis=2)
    mixed = jnp.einsum(
        "hqk,khd->qhd", weights.astype(jnp.bfloat16), values, preferred_element_type=jnp.float32
    )
    return (mixed / jnp.transpose(total)[:, :, None]).astype(jnp.bfloat16)


def prefill_attend(query, fresh_key, fresh_value, prior, offset):
    count, heads = (query.shape[0], query.shape[1])
    capacity = prior.shape[1]
    keys = jnp.concatenate([prior[0].reshape(capacity, heads, HD), fresh_key], axis=0)
    values = jnp.concatenate([prior[1].reshape(capacity, heads, HD), fresh_value], axis=0)
    block = min(count, 512)

    def one_block(start):
        places = start + jnp.arange(block, dtype=jnp.int32)
        live = jnp.concatenate(
            [
                jnp.broadcast_to(jnp.arange(capacity)[None, :] < offset, (block, capacity)),
                jnp.arange(count)[None, :] <= places[:, None],
            ],
            axis=1,
        )
        return attend_rows(query, keys, values, live)

    starts = jnp.arange(count // block, dtype=jnp.int32) * block
    return lax.map(one_block, starts).reshape(count, heads * HD)


def piece_rows(query, keys, values, live):
    count, heads = query.shape[0], query.shape[1]
    own = jnp.arange(heads)[:, None] == jnp.arange(heads)[None, :]
    spread = jnp.where(own[None, :, None, :], query[:, :, :, None], jnp.zeros((), query.dtype))
    spread = spread.reshape(count, heads * HD, heads)
    scores = jnp.einsum("rkf,rfh->rhk", keys, spread, preferred_element_type=jnp.float32) * (
        1.0 / math.sqrt(HD)
    )
    masked = jnp.where(live[:, None, :], scores, NEG)
    highest = jnp.max(masked, axis=2)
    weights = jnp.where(live[:, None, :], jnp.exp(masked - highest[:, :, None]), 0.0)
    total = jnp.sum(weights, axis=2)
    mixed = jnp.einsum(
        "rhk,rkf->rhf", weights.astype(jnp.bfloat16), values, preferred_element_type=jnp.float32
    ).reshape(count, heads, heads, HD)
    summed = jnp.sum(jnp.where(own[None, :, :, None], mixed, 0.0), axis=2)
    return (highest, total, summed)


def piece_batch(query, store, lengths):
    capacity = store.shape[2]
    live = jnp.arange(capacity)[None, :] < lengths[:, None]
    return piece_rows(query, store[:, 0], store[:, 1], live)


def home_partial(query, fresh_key, fresh_value, cache, lengths):
    count, capacity = (cache.shape[0], cache.shape[2])
    keys = jnp.concatenate([cache[:, 0], fresh_key.reshape(count, 1, -1)], axis=1)
    values = jnp.concatenate([cache[:, 1], fresh_value.reshape(count, 1, -1)], axis=1)
    live = jnp.concatenate(
        [jnp.arange(capacity)[None, :] < lengths[:, None], jnp.ones((count, 1), jnp.bool_)], axis=1
    )
    return piece_rows(query, keys, values, live)


def combine(parts):
    highest = reduce(jnp.maximum, [part[0] for part in parts])
    factors = [jnp.exp(part[0] - highest) for part in parts]
    upper = reduce(jnp.add, [factor[:, :, None] * part[2] for factor, part in zip(factors, parts)])
    lower = reduce(jnp.add, [factor * part[1] for factor, part in zip(factors, parts)])
    return (upper / lower[:, :, None]).astype(jnp.bfloat16)


def local(
    prefill_x,
    decode_x,
    ln_gain,
    ln_bias,
    qkv_weight,
    qkv_bias,
    prior_cache,
    prefill_offset,
    home_cache,
    piece_len,
    side_store,
):
    count = prefill_x.shape[0]
    requests = decode_x.shape[0]
    groups = lax.axis_size("group")
    forward = [(i, (i + 1) % groups) for i in range(groups)]
    backward = [((i + 1) % groups, i) for i in range(groups)]
    mine = jnp.concatenate([decode_x.astype(jnp.float32), piece_len.astype(jnp.float32)], axis=1)
    width = decode_x.shape[1]

    def neighbour(pairs):
        got = lax.ppermute(mine, "group", pairs)
        return got[:, :width].astype(decode_x.dtype), got[:, width:].astype(jnp.int32)

    prev_x, prev_len = neighbour(forward)
    next_x, next_len = neighbour(backward)
    rows = jnp.concatenate([prefill_x, decode_x, prev_x, next_x], axis=0)
    ring = lax.axis_size("ty")
    y = lax.axis_index("ty")
    z = lax.axis_index("tz")
    up = [(i, (i + 1) % ring) for i in range(ring)]
    down = [(i, (i - 1) % ring) for i in range(ring)]
    half = rows.shape[0] // 2

    def around(block):
        below = lax.ppermute(block, "ty", up)
        above = lax.ppermute(block, "ty", down)
        across = jnp.concatenate(
            [lax.ppermute(below[:half], "ty", up), lax.ppermute(above[half:], "ty", down)], axis=0
        )
        return [block, below, above, across]

    partner = lax.ppermute(rows, "tz", [(0, 1), (1, 0)])
    pieces = around(rows) + around(partner)
    whole = jnp.concatenate(pieces, axis=1)
    spots = jnp.stack([y, (y + ring - 1) % ring, (y + 1) % ring, (y + 2) % ring])
    order = jnp.concatenate([spots * 2 + z, spots * 2 + (1 - z)]).astype(jnp.int32)

    def feature_order(table):
        return table.reshape(order.shape[0], -1)[order].reshape(table.shape)

    gain, shift = feature_order(ln_gain), feature_order(ln_bias)
    weight = jnp.transpose(qkv_weight, (1, 0, 2))
    lengths = jnp.concatenate([piece_len, prev_len, next_len], axis=0)
    all_query, all_key, all_value = project(
        layer_norm(whole[count:], gain, shift),
        weight,
        qkv_bias,
        lengths[:, 0] + lengths[:, 1] + lengths[:, 2],
        order,
    )
    own_query = all_query[:requests]
    prev_query = all_query[requests : 2 * requests]
    next_query = all_query[2 * requests :]
    home_parts = home_partial(
        own_query, all_key[:requests], all_value[:requests], home_cache, piece_len[:, 1]
    )

    def answer(parts, pairs):
        highest, total, summed = parts
        packed = jnp.concatenate([summed, highest[:, :, None], total[:, :, None]], axis=2)
        got = lax.ppermute(packed, "group", pairs)
        return (got[:, :, HD], got[:, :, HD + 1], got[:, :, :HD])

    right_for_prev = piece_batch(prev_query, side_store[:requests], prev_len[:, 2])
    left_for_next = piece_batch(next_query, side_store[requests:], next_len[:, 0])
    right_parts, left_parts, normed = lax.optimization_barrier(
        (
            answer(right_for_prev, backward),
            answer(left_for_next, forward),
            layer_norm(whole[:count], gain, shift),
        )
    )
    query, fresh_key, fresh_value = project(
        normed,
        weight,
        qkv_bias,
        prefill_offset[0] + jnp.arange(count, dtype=jnp.int32),
        order,
    )
    prefill_out = prefill_attend(query, fresh_key, fresh_value, prior_cache[0], prefill_offset[0])
    decode_out = combine([left_parts, home_parts, right_parts]).reshape(requests, -1)
    return (prefill_out, decode_out)


def solution(mesh):
    devices = mesh.devices.reshape(mesh.devices.shape[0], -1, 2)
    split = jax.sharding.Mesh(devices, ("group", "ty", "tz"))
    tp = ("ty", "tz")
    inner = jax.shard_map(
        local,
        mesh=split,
        in_specs=(
            P("group", tp),
            P("group", tp),
            P(),
            P(),
            P(None, None, tp),
            P(None, tp),
            P("group", None, None, tp),
            P("group"),
            P("group", None, None, tp),
            P("group", None),
            P("group", None, None, tp),
        ),
        out_specs=(P("group", tp), P("group", tp)),
        check_vma=False,
    )
    return inner
```

```python
from functools import reduce
import math

import jax
import jax.numpy as jnp
from jax import lax
from jax.experimental import pallas as pl
from jax.experimental.pallas import tpu as pltpu
from jax.sharding import PartitionSpec as P

HD = 128
ROT = 32


EPS = 1e-05
NEG = -1e30


def with_halo(block, sides, width):
    for axis, dim in sides:
        count = lax.axis_size(axis)
        forward = [(i, i + 1) for i in range(count - 1)]
        forward.append((count - 1, 0))
        backward = [(target, source) for source, target in forward]
        low = lax.ppermute(
            lax.slice_in_dim(block, block.shape[dim] - width, None, axis=dim), axis, forward
        )
        high = lax.ppermute(lax.slice_in_dim(block, 0, width, axis=dim), axis, backward)
        block = jnp.concatenate([low, block, high], axis=dim)
    return block


def layer_norm(rows, gain, shift):
    rows = rows.astype(jnp.float32)
    middle = jnp.mean(rows, axis=-1, keepdims=True)
    centred = rows - middle
    spread = jnp.mean(centred * centred, axis=-1, keepdims=True)
    return (centred * lax.rsqrt(spread + EPS) * gain + shift).astype(jnp.bfloat16)


def rotate(vectors, positions):
    half = ROT // 2
    steps = jnp.arange(half, dtype=jnp.float32) * (2.0 / ROT)
    frequency = jnp.exp(-math.log(10000.0) * steps)
    angle = positions.astype(jnp.float32)[:, None] * frequency[None, :]
    cosine = jnp.cos(angle)[:, None, :]
    sine = jnp.sin(angle)[:, None, :]
    first = vectors[..., :half]
    second = vectors[..., half:ROT]
    return jnp.concatenate(
        [first * cosine - second * sine, second * cosine + first * sine, vectors[..., ROT:]],
        axis=-1,
    )


def qkv_kernel(order_ref, x_ref, gain_ref, shift_ref, w_ref, o_ref):
    rows = x_ref[...].astype(jnp.float32)
    middle = jnp.mean(rows, axis=-1, keepdims=True)
    centred = rows - middle
    spread = jnp.mean(centred * centred, axis=-1, keepdims=True)
    normed = (centred * lax.rsqrt(spread + EPS) * gain_ref[...] + shift_ref[...]).astype(
        jnp.bfloat16
    )
    parts, depth, width = w_ref.shape
    blocks = order_ref.shape[0]
    size = depth // blocks
    for c in range(parts):
        total = jnp.zeros((rows.shape[0], width), jnp.float32)
        for j in range(blocks):
            start = pl.multiple_of(order_ref[j] * size, size)
            total += jnp.dot(
                normed[:, j * size : (j + 1) * size],
                w_ref[c, pl.ds(start, size), :],
                preferred_element_type=jnp.float32,
            )
        o_ref[:, c * width : (c + 1) * width] = total


def qkv_matmul(whole, gain, shift, weight, order):
    rows, depth = whole.shape
    parts, _, width = weight.shape
    chunk = 128 if rows % 128 == 0 else rows
    return pl.pallas_call(
        qkv_kernel,
        out_shape=jax.ShapeDtypeStruct((rows, parts * width), jnp.float32),
        grid_spec=pltpu.PrefetchScalarGridSpec(
            num_scalar_prefetch=1,
            grid=(rows // chunk,),
            in_specs=[
                pl.BlockSpec((chunk, depth), lambda i, order: (i, 0)),
                pl.BlockSpec((1, depth), lambda i, order: (0, 0)),
                pl.BlockSpec((1, depth), lambda i, order: (0, 0)),
                pl.BlockSpec((parts, depth, width), lambda i, order: (0, 0, 0)),
            ],
            out_specs=pl.BlockSpec((chunk, parts * width), lambda i, order: (i, 0)),
        ),
        compiler_params=pltpu.CompilerParams(
            dimension_semantics=("arbitrary",), vmem_limit_bytes=48 * 1024 * 1024
        ),
        cost_estimate=pl.CostEstimate(
            flops=2 * rows * depth * parts * width,
            bytes_accessed=2 * rows * depth + 2 * depth * parts * width + 4 * rows * parts * width,
            transcendentals=rows,
        ),
    )(order, whole, gain.reshape(1, depth), shift.reshape(1, depth), weight)


def project(whole, gain, shift, weight, bias, positions, order):
    count = whole.shape[0]
    width = weight.shape[2]
    mixed = qkv_matmul(whole, gain, shift, weight, order)
    mixed = (mixed + bias.reshape(1, 3 * width)).reshape(count, 3, width // HD, HD)
    query = rotate(mixed[:, 0], positions).astype(jnp.bfloat16)
    fresh_key = rotate(mixed[:, 1], positions).astype(jnp.bfloat16)
    fresh_value = mixed[:, 2].astype(jnp.bfloat16)
    return (query, fresh_key, fresh_value)


def attend_rows(query, keys, values, live):
    scores = jnp.einsum("qhd,khd->hqk", query, keys, preferred_element_type=jnp.float32) * (
        1.0 / math.sqrt(HD)
    )
    masked = jnp.where(live[None], scores, NEG)
    highest = jnp.max(masked, axis=2, keepdims=True)
    weights = jnp.where(live[None], jnp.exp(masked - highest), 0.0)
    total = jnp.sum(weights, axis=2)
    mixed = jnp.einsum(
        "hqk,khd->qhd", weights.astype(jnp.bfloat16), values, preferred_element_type=jnp.float32
    )
    return (mixed / jnp.transpose(total)[:, :, None]).astype(jnp.bfloat16)


def prefill_attend(query, fresh_key, fresh_value, prior, offset):
    count, heads = (query.shape[0], query.shape[1])
    capacity = prior.shape[1]
    keys = jnp.concatenate([prior[0].reshape(capacity, heads, HD), fresh_key], axis=0)
    values = jnp.concatenate([prior[1].reshape(capacity, heads, HD), fresh_value], axis=0)
    block = min(count, 512)

    def one_block(start):
        places = start + jnp.arange(block, dtype=jnp.int32)
        live = jnp.concatenate(
            [
                jnp.broadcast_to(jnp.arange(capacity)[None, :] < offset, (block, capacity)),
                jnp.arange(count)[None, :] <= places[:, None],
            ],
            axis=1,
        )
        return attend_rows(query, keys, values, live)

    starts = jnp.arange(count // block, dtype=jnp.int32) * block
    return lax.map(one_block, starts).reshape(count, heads * HD)


def piece_rows(query, keys, values, live):
    count, heads = query.shape[0], query.shape[1]
    own = jnp.arange(heads)[:, None] == jnp.arange(heads)[None, :]
    spread = jnp.where(own[None, :, None, :], query[:, :, :, None], jnp.zeros((), query.dtype))
    spread = spread.reshape(count, heads * HD, heads)
    scores = jnp.einsum("rkf,rfh->rhk", keys, spread, preferred_element_type=jnp.float32) * (
        1.0 / math.sqrt(HD)
    )
    masked = jnp.where(live[:, None, :], scores, NEG)
    highest = jnp.max(masked, axis=2)
    weights = jnp.where(live[:, None, :], jnp.exp(masked - highest[:, :, None]), 0.0)
    total = jnp.sum(weights, axis=2)
    mixed = jnp.einsum(
        "rhk,rkf->rhf", weights.astype(jnp.bfloat16), values, preferred_element_type=jnp.float32
    ).reshape(count, heads, heads, HD)
    summed = jnp.sum(jnp.where(own[None, :, :, None], mixed, 0.0), axis=2)
    return (highest, total, summed)


def piece_batch(query, store, lengths):
    capacity = store.shape[2]
    live = jnp.arange(capacity)[None, :] < lengths[:, None]
    return piece_rows(query, store[:, 0], store[:, 1], live)


def home_partial(query, fresh_key, fresh_value, cache, lengths):
    count, capacity = (cache.shape[0], cache.shape[2])
    keys = jnp.concatenate([cache[:, 0], fresh_key.reshape(count, 1, -1)], axis=1)
    values = jnp.concatenate([cache[:, 1], fresh_value.reshape(count, 1, -1)], axis=1)
    live = jnp.concatenate(
        [jnp.arange(capacity)[None, :] < lengths[:, None], jnp.ones((count, 1), jnp.bool_)], axis=1
    )
    return piece_rows(query, keys, values, live)


def combine(parts):
    highest = reduce(jnp.maximum, [part[0] for part in parts])
    factors = [jnp.exp(part[0] - highest) for part in parts]
    upper = reduce(jnp.add, [factor[:, :, None] * part[2] for factor, part in zip(factors, parts)])
    lower = reduce(jnp.add, [factor * part[1] for factor, part in zip(factors, parts)])
    return (upper / lower[:, :, None]).astype(jnp.bfloat16)


def local(
    prefill_x,
    decode_x,
    ln_gain,
    ln_bias,
    qkv_weight,
    qkv_bias,
    prior_cache,
    prefill_offset,
    home_cache,
    piece_len,
    side_store,
):
    count = prefill_x.shape[0]
    requests = decode_x.shape[0]
    rows = jnp.concatenate([prefill_x, decode_x], axis=0)
    ring = lax.axis_size("ty")
    y = lax.axis_index("ty")
    z = lax.axis_index("tz")
    up = [(i, (i + 1) % ring) for i in range(ring)]
    down = [(i, (i - 1) % ring) for i in range(ring)]
    half = rows.shape[0] // 2

    def around(block):
        below = lax.ppermute(block, "ty", up)
        above = lax.ppermute(block, "ty", down)
        across = jnp.concatenate(
            [lax.ppermute(below[:half], "ty", up), lax.ppermute(above[half:], "ty", down)], axis=0
        )
        return [block, below, above, across]

    partner = lax.ppermute(rows, "tz", [(0, 1), (1, 0)])
    pieces = around(rows) + around(partner)
    whole = jnp.concatenate(pieces, axis=1)
    spots = jnp.stack([y, (y + ring - 1) % ring, (y + 1) % ring, (y + 2) % ring])
    order = jnp.concatenate([spots * 2 + z, spots * 2 + (1 - z)]).astype(jnp.int32)

    def feature_order(table):
        return table.reshape(order.shape[0], -1)[order].reshape(table.shape)

    gain, shift = feature_order(ln_gain), feature_order(ln_bias)
    weight = jnp.transpose(qkv_weight, (1, 0, 2))
    own_query, new_key, new_value = project(
        whole[count:],
        gain,
        shift,
        weight,
        qkv_bias,
        piece_len[:, 0] + piece_len[:, 1] + piece_len[:, 2],
        order,
    )
    home_parts = home_partial(own_query, new_key, new_value, home_cache, piece_len[:, 1])
    groups = lax.axis_size("group")
    forward = [(i, (i + 1) % groups) for i in range(groups)]
    backward = [((i + 1) % groups, i) for i in range(groups)]
    heads = own_query.shape[1]

    def ask(lengths, pairs):
        packed = jnp.concatenate(
            [own_query.astype(jnp.float32).reshape(requests, -1), lengths[:, None].astype(jnp.float32)],
            axis=1,
        )
        got = lax.ppermute(packed, "group", pairs)
        return got[:, :-1].reshape(own_query.shape).astype(own_query.dtype), got[:, -1].astype(jnp.int32)

    def answer(parts, pairs):
        highest, total, summed = parts
        packed = jnp.concatenate([summed, highest[:, :, None], total[:, :, None]], axis=2)
        got = lax.ppermute(packed, "group", pairs)
        return (got[:, :, HD], got[:, :, HD + 1], got[:, :, :HD])

    prev_query, prev_len = ask(piece_len[:, 2], forward)
    next_query, next_len = ask(piece_len[:, 0], backward)
    right_parts = answer(piece_batch(prev_query, side_store[:requests], prev_len), backward)
    left_parts = answer(piece_batch(next_query, side_store[requests:], next_len), forward)
    query, fresh_key, fresh_value = project(
        whole[:count],
        gain,
        shift,
        weight,
        qkv_bias,
        prefill_offset[0] + jnp.arange(count, dtype=jnp.int32),
        order,
    )
    prefill_out = prefill_attend(query, fresh_key, fresh_value, prior_cache[0], prefill_offset[0])
    decode_out = combine([left_parts, home_parts, right_parts]).reshape(requests, -1)
    return (prefill_out, decode_out)


def solution(mesh):
    devices = mesh.devices.reshape(mesh.devices.shape[0], -1, 2)
    split = jax.sharding.Mesh(devices, ("group", "ty", "tz"))
    tp = ("ty", "tz")
    inner = jax.shard_map(
        local,
        mesh=split,
        in_specs=(
            P("group", tp),
            P("group", tp),
            P(),
            P(),
            P(None, None, tp),
            P(None, tp),
            P("group", None, None, tp),
            P("group"),
            P("group", None, None, tp),
            P("group", None),
            P("group", None, None, tp),
        ),
        out_specs=(P("group", tp), P("group", tp)),
        check_vma=False,
    )
    return inner
```

```python
from functools import reduce
import math

import jax
import jax.numpy as jnp
from jax import lax
from jax.experimental import pallas as pl
from jax.experimental.pallas import tpu as pltpu
from jax.sharding import PartitionSpec as P

HD = 128
ROT = 32


EPS = 1e-05
NEG = -1e30


def with_halo(block, sides, width):
    for axis, dim in sides:
        count = lax.axis_size(axis)
        forward = [(i, i + 1) for i in range(count - 1)]
        forward.append((count - 1, 0))
        backward = [(target, source) for source, target in forward]
        low = lax.ppermute(
            lax.slice_in_dim(block, block.shape[dim] - width, None, axis=dim), axis, forward
        )
        high = lax.ppermute(lax.slice_in_dim(block, 0, width, axis=dim), axis, backward)
        block = jnp.concatenate([low, block, high], axis=dim)
    return block


def layer_norm(rows, gain, shift):
    rows = rows.astype(jnp.float32)
    middle = jnp.mean(rows, axis=-1, keepdims=True)
    centred = rows - middle
    spread = jnp.mean(centred * centred, axis=-1, keepdims=True)
    return (centred * lax.rsqrt(spread + EPS) * gain + shift).astype(jnp.bfloat16)


def rotate(vectors, positions):
    half = ROT // 2
    steps = jnp.arange(half, dtype=jnp.float32) * (2.0 / ROT)
    frequency = jnp.exp(-math.log(10000.0) * steps)
    angle = positions.astype(jnp.float32)[:, None] * frequency[None, :]
    cosine = jnp.cos(angle)[:, None, :]
    sine = jnp.sin(angle)[:, None, :]
    first = vectors[..., :half]
    second = vectors[..., half:ROT]
    return jnp.concatenate(
        [first * cosine - second * sine, second * cosine + first * sine, vectors[..., ROT:]],
        axis=-1,
    )


def qkv_kernel(order_ref, x_ref, gain_ref, shift_ref, w_ref, o_ref):
    rows = x_ref[...].astype(jnp.float32)
    middle = jnp.mean(rows, axis=-1, keepdims=True)
    centred = rows - middle
    spread = jnp.mean(centred * centred, axis=-1, keepdims=True)
    normed = (centred * lax.rsqrt(spread + EPS) * gain_ref[...] + shift_ref[...]).astype(
        jnp.bfloat16
    )
    parts, depth, width = w_ref.shape
    blocks = order_ref.shape[0]
    size = depth // blocks
    for c in range(parts):
        total = jnp.zeros((rows.shape[0], width), jnp.float32)
        for j in range(blocks):
            start = pl.multiple_of(order_ref[j] * size, size)
            total += jnp.dot(
                normed[:, j * size : (j + 1) * size],
                w_ref[c, pl.ds(start, size), :],
                preferred_element_type=jnp.float32,
            )
        o_ref[:, c * width : (c + 1) * width] = total


def qkv_matmul(whole, first, rows, gain, shift, weight, order):
    depth = whole.shape[1]
    parts, _, width = weight.shape
    chunk = 128 if rows % 128 == 0 else rows
    skip = first // chunk
    return pl.pallas_call(
        qkv_kernel,
        out_shape=jax.ShapeDtypeStruct((rows, parts * width), jnp.float32),
        grid_spec=pltpu.PrefetchScalarGridSpec(
            num_scalar_prefetch=1,
            grid=(rows // chunk,),
            in_specs=[
                pl.BlockSpec((chunk, depth), lambda i, order: (i + skip, 0)),
                pl.BlockSpec((1, depth), lambda i, order: (0, 0)),
                pl.BlockSpec((1, depth), lambda i, order: (0, 0)),
                pl.BlockSpec((parts, depth, width), lambda i, order: (0, 0, 0)),
            ],
            out_specs=pl.BlockSpec((chunk, parts * width), lambda i, order: (i, 0)),
        ),
        compiler_params=pltpu.CompilerParams(
            dimension_semantics=("arbitrary",), vmem_limit_bytes=48 * 1024 * 1024
        ),
        cost_estimate=pl.CostEstimate(
            flops=2 * rows * depth * parts * width,
            bytes_accessed=2 * rows * depth + 2 * depth * parts * width + 4 * rows * parts * width,
            transcendentals=rows,
        ),
    )(order, whole, gain.reshape(1, depth), shift.reshape(1, depth), weight)


def project(whole, first, count, gain, shift, weight, bias, positions, order):
    width = weight.shape[2]
    mixed = qkv_matmul(whole, first, count, gain, shift, weight, order)
    mixed = (mixed + bias.reshape(1, 3 * width)).reshape(count, 3, width // HD, HD)
    query = rotate(mixed[:, 0], positions).astype(jnp.bfloat16)
    fresh_key = rotate(mixed[:, 1], positions).astype(jnp.bfloat16)
    fresh_value = mixed[:, 2].astype(jnp.bfloat16)
    return (query, fresh_key, fresh_value)


def attend_rows(query, keys, values, live):
    scores = jnp.einsum("qhd,khd->hqk", query, keys, preferred_element_type=jnp.float32) * (
        1.0 / math.sqrt(HD)
    )
    masked = jnp.where(live[None], scores, NEG)
    highest = jnp.max(masked, axis=2, keepdims=True)
    weights = jnp.where(live[None], jnp.exp(masked - highest), 0.0)
    total = jnp.sum(weights, axis=2)
    mixed = jnp.einsum(
        "hqk,khd->qhd", weights.astype(jnp.bfloat16), values, preferred_element_type=jnp.float32
    )
    return (mixed / jnp.transpose(total)[:, :, None]).astype(jnp.bfloat16)


def prefill_attend(query, fresh_key, fresh_value, prior, offset):
    count, heads = (query.shape[0], query.shape[1])
    capacity = prior.shape[1]
    keys = jnp.concatenate([prior[0].reshape(capacity, heads, HD), fresh_key], axis=0)
    values = jnp.concatenate([prior[1].reshape(capacity, heads, HD), fresh_value], axis=0)
    block = min(count, 512)

    def one_block(start):
        places = start + jnp.arange(block, dtype=jnp.int32)
        live = jnp.concatenate(
            [
                jnp.broadcast_to(jnp.arange(capacity)[None, :] < offset, (block, capacity)),
                jnp.arange(count)[None, :] <= places[:, None],
            ],
            axis=1,
        )
        return attend_rows(query, keys, values, live)

    starts = jnp.arange(count // block, dtype=jnp.int32) * block
    return lax.map(one_block, starts).reshape(count, heads * HD)


def piece_rows(query, keys, values, live):
    count, heads = query.shape[0], query.shape[1]
    own = jnp.arange(heads)[:, None] == jnp.arange(heads)[None, :]
    spread = jnp.where(own[None, :, None, :], query[:, :, :, None], jnp.zeros((), query.dtype))
    spread = spread.reshape(count, heads * HD, heads)
    scores = jnp.einsum("rkf,rfh->rhk", keys, spread, preferred_element_type=jnp.float32) * (
        1.0 / math.sqrt(HD)
    )
    masked = jnp.where(live[:, None, :], scores, NEG)
    highest = jnp.max(masked, axis=2)
    weights = jnp.where(live[:, None, :], jnp.exp(masked - highest[:, :, None]), 0.0)
    total = jnp.sum(weights, axis=2)
    mixed = jnp.einsum(
        "rhk,rkf->rhf", weights.astype(jnp.bfloat16), values, preferred_element_type=jnp.float32
    ).reshape(count, heads, heads, HD)
    summed = jnp.sum(jnp.where(own[None, :, :, None], mixed, 0.0), axis=2)
    return (highest, total, summed)


def piece_batch(query, store, lengths):
    capacity = store.shape[2]
    live = jnp.arange(capacity)[None, :] < lengths[:, None]
    return piece_rows(query, store[:, 0], store[:, 1], live)


def home_partial(query, fresh_key, fresh_value, cache, lengths):
    count, capacity = (cache.shape[0], cache.shape[2])
    keys = jnp.concatenate([cache[:, 0], fresh_key.reshape(count, 1, -1)], axis=1)
    values = jnp.concatenate([cache[:, 1], fresh_value.reshape(count, 1, -1)], axis=1)
    live = jnp.concatenate(
        [jnp.arange(capacity)[None, :] < lengths[:, None], jnp.ones((count, 1), jnp.bool_)], axis=1
    )
    return piece_rows(query, keys, values, live)


def combine(parts):
    highest = reduce(jnp.maximum, [part[0] for part in parts])
    factors = [jnp.exp(part[0] - highest) for part in parts]
    upper = reduce(jnp.add, [factor[:, :, None] * part[2] for factor, part in zip(factors, parts)])
    lower = reduce(jnp.add, [factor * part[1] for factor, part in zip(factors, parts)])
    return (upper / lower[:, :, None]).astype(jnp.bfloat16)


def local(
    prefill_x,
    decode_x,
    ln_gain,
    ln_bias,
    qkv_weight,
    qkv_bias,
    prior_cache,
    prefill_offset,
    home_cache,
    piece_len,
    side_store,
):
    count = prefill_x.shape[0]
    requests = decode_x.shape[0]
    rows = jnp.concatenate([prefill_x, decode_x], axis=0)
    ring = lax.axis_size("ty")
    y = lax.axis_index("ty")
    z = lax.axis_index("tz")
    up = [(i, (i + 1) % ring) for i in range(ring)]
    down = [(i, (i - 1) % ring) for i in range(ring)]
    half = rows.shape[0] // 2

    def around(block):
        below = lax.ppermute(block, "ty", up)
        above = lax.ppermute(block, "ty", down)
        across = jnp.concatenate(
            [lax.ppermute(below[:half], "ty", up), lax.ppermute(above[half:], "ty", down)], axis=0
        )
        return [block, below, above, across]

    partner = lax.ppermute(rows, "tz", [(0, 1), (1, 0)])
    pieces = around(rows) + around(partner)
    whole = jnp.concatenate(pieces, axis=1)
    spots = jnp.stack([y, (y + ring - 1) % ring, (y + 1) % ring, (y + 2) % ring])
    order = jnp.concatenate([spots * 2 + z, spots * 2 + (1 - z)]).astype(jnp.int32)

    def feature_order(table):
        return table.reshape(order.shape[0], -1)[order].reshape(table.shape)

    gain, shift = feature_order(ln_gain), feature_order(ln_bias)
    weight = jnp.transpose(qkv_weight, (1, 0, 2))
    own_query, new_key, new_value = project(
        whole[count:],
        0,
        requests,
        gain,
        shift,
        weight,
        qkv_bias,
        piece_len[:, 0] + piece_len[:, 1] + piece_len[:, 2],
        order,
    )
    home_parts = home_partial(own_query, new_key, new_value, home_cache, piece_len[:, 1])
    groups = lax.axis_size("group")
    forward = [(i, (i + 1) % groups) for i in range(groups)]
    backward = [((i + 1) % groups, i) for i in range(groups)]
    heads = own_query.shape[1]

    def ask(lengths, pairs):
        packed = jnp.concatenate(
            [own_query.astype(jnp.float32).reshape(requests, -1), lengths[:, None].astype(jnp.float32)],
            axis=1,
        )
        got = lax.ppermute(packed, "group", pairs)
        return got[:, :-1].reshape(own_query.shape).astype(own_query.dtype), got[:, -1].astype(jnp.int32)

    def answer(parts, pairs):
        highest, total, summed = parts
        packed = jnp.concatenate([summed, highest[:, :, None], total[:, :, None]], axis=2)
        got = lax.ppermute(packed, "group", pairs)
        return (got[:, :, HD], got[:, :, HD + 1], got[:, :, :HD])

    prev_query, prev_len = ask(piece_len[:, 2], forward)
    next_query, next_len = ask(piece_len[:, 0], backward)
    right_parts = answer(piece_batch(prev_query, side_store[:requests], prev_len), backward)
    left_parts = answer(piece_batch(next_query, side_store[requests:], next_len), forward)
    query, fresh_key, fresh_value = project(
        whole,
        0,
        count,
        gain,
        shift,
        weight,
        qkv_bias,
        prefill_offset[0] + jnp.arange(count, dtype=jnp.int32),
        order,
    )
    prefill_out = prefill_attend(query, fresh_key, fresh_value, prior_cache[0], prefill_offset[0])
    decode_out = combine([left_parts, home_parts, right_parts]).reshape(requests, -1)
    return (prefill_out, decode_out)


def solution(mesh):
    devices = mesh.devices.reshape(mesh.devices.shape[0], -1, 2)
    split = jax.sharding.Mesh(devices, ("group", "ty", "tz"))
    tp = ("ty", "tz")
    inner = jax.shard_map(
        local,
        mesh=split,
        in_specs=(
            P("group", tp),
            P("group", tp),
            P(),
            P(),
            P(None, None, tp),
            P(None, tp),
            P("group", None, None, tp),
            P("group"),
            P("group", None, None, tp),
            P("group", None),
            P("group", None, None, tp),
        ),
        out_specs=(P("group", tp), P("group", tp)),
        check_vma=False,
    )
    return inner
```

```python
from functools import reduce
import math

import jax
import jax.numpy as jnp
from jax import lax
from jax.experimental import pallas as pl
from jax.experimental.pallas import tpu as pltpu
from jax.sharding import PartitionSpec as P

HD = 128
ROT = 32


EPS = 1e-05
NEG = -1e30


def with_halo(block, sides, width):
    for axis, dim in sides:
        count = lax.axis_size(axis)
        forward = [(i, i + 1) for i in range(count - 1)]
        forward.append((count - 1, 0))
        backward = [(target, source) for source, target in forward]
        low = lax.ppermute(
            lax.slice_in_dim(block, block.shape[dim] - width, None, axis=dim), axis, forward
        )
        high = lax.ppermute(lax.slice_in_dim(block, 0, width, axis=dim), axis, backward)
        block = jnp.concatenate([low, block, high], axis=dim)
    return block


def layer_norm(rows, gain, shift):
    rows = rows.astype(jnp.float32)
    middle = jnp.mean(rows, axis=-1, keepdims=True)
    centred = rows - middle
    spread = jnp.mean(centred * centred, axis=-1, keepdims=True)
    return (centred * lax.rsqrt(spread + EPS) * gain + shift).astype(jnp.bfloat16)


def rotate(vectors, positions):
    half = ROT // 2
    steps = jnp.arange(half, dtype=jnp.float32) * (2.0 / ROT)
    frequency = jnp.exp(-math.log(10000.0) * steps)
    angle = positions.astype(jnp.float32)[:, None] * frequency[None, :]
    cosine = jnp.cos(angle)[:, None, :]
    sine = jnp.sin(angle)[:, None, :]
    first = vectors[..., :half]
    second = vectors[..., half:ROT]
    return jnp.concatenate(
        [first * cosine - second * sine, second * cosine + first * sine, vectors[..., ROT:]],
        axis=-1,
    )


def qkv_kernel(order_ref, x_ref, gain_ref, shift_ref, w_ref, o_ref):
    rows = x_ref[...].astype(jnp.float32)
    middle = jnp.mean(rows, axis=-1, keepdims=True)
    centred = rows - middle
    spread = jnp.mean(centred * centred, axis=-1, keepdims=True)
    normed = (centred * lax.rsqrt(spread + EPS) * gain_ref[...] + shift_ref[...]).astype(
        jnp.bfloat16
    )
    parts, depth, width = w_ref.shape
    blocks = order_ref.shape[0]
    size = depth // blocks
    for c in range(parts):
        total = jnp.zeros((rows.shape[0], width), jnp.float32)
        for j in range(blocks):
            start = pl.multiple_of(order_ref[j] * size, size)
            total += jnp.dot(
                normed[:, j * size : (j + 1) * size],
                w_ref[c, pl.ds(start, size), :],
                preferred_element_type=jnp.float32,
            )
        o_ref[:, c * width : (c + 1) * width] = total


def qkv_matmul(whole, first, rows, gain, shift, weight, order):
    depth = whole.shape[1]
    parts, _, width = weight.shape
    chunk = 128 if rows % 128 == 0 else rows
    skip = first // chunk
    return pl.pallas_call(
        qkv_kernel,
        out_shape=jax.ShapeDtypeStruct((rows, parts * width), jnp.float32),
        grid_spec=pltpu.PrefetchScalarGridSpec(
            num_scalar_prefetch=1,
            grid=(rows // chunk,),
            in_specs=[
                pl.BlockSpec((chunk, depth), lambda i, order: (i + skip, 0)),
                pl.BlockSpec((1, depth), lambda i, order: (0, 0)),
                pl.BlockSpec((1, depth), lambda i, order: (0, 0)),
                pl.BlockSpec((parts, depth, width), lambda i, order: (0, 0, 0)),
            ],
            out_specs=pl.BlockSpec((chunk, parts * width), lambda i, order: (i, 0)),
        ),
        compiler_params=pltpu.CompilerParams(
            dimension_semantics=("arbitrary",), vmem_limit_bytes=48 * 1024 * 1024
        ),
        cost_estimate=pl.CostEstimate(
            flops=2 * rows * depth * parts * width,
            bytes_accessed=2 * rows * depth + 2 * depth * parts * width + 4 * rows * parts * width,
            transcendentals=rows,
        ),
    )(order, whole, gain.reshape(1, depth), shift.reshape(1, depth), weight)


def project(whole, first, count, gain, shift, weight, bias, positions, order):
    width = weight.shape[2]
    mixed = qkv_matmul(whole, first, count, gain, shift, weight, order)
    mixed = (mixed + bias.reshape(1, 3 * width)).reshape(count, 3, width // HD, HD)
    query = rotate(mixed[:, 0], positions).astype(jnp.bfloat16)
    fresh_key = rotate(mixed[:, 1], positions).astype(jnp.bfloat16)
    fresh_value = mixed[:, 2].astype(jnp.bfloat16)
    return (query, fresh_key, fresh_value)


def attend_rows(query, keys, values, live):
    scores = jnp.einsum("qhd,khd->hqk", query, keys, preferred_element_type=jnp.float32) * (
        1.0 / math.sqrt(HD)
    )
    masked = jnp.where(live[None], scores, NEG)
    highest = jnp.max(masked, axis=2, keepdims=True)
    weights = jnp.where(live[None], jnp.exp(masked - highest), 0.0)
    total = jnp.sum(weights, axis=2)
    mixed = jnp.einsum(
        "hqk,khd->qhd", weights.astype(jnp.bfloat16), values, preferred_element_type=jnp.float32
    )
    return (mixed / jnp.transpose(total)[:, :, None]).astype(jnp.bfloat16)


def prefill_attend(query, fresh_key, fresh_value, prior, offset):
    count, heads = (query.shape[0], query.shape[1])
    capacity = prior.shape[1]
    keys = jnp.concatenate([prior[0].reshape(capacity, heads, HD), fresh_key], axis=0)
    values = jnp.concatenate([prior[1].reshape(capacity, heads, HD), fresh_value], axis=0)
    block = min(count, 512)

    def one_block(start):
        places = start + jnp.arange(block, dtype=jnp.int32)
        live = jnp.concatenate(
            [
                jnp.broadcast_to(jnp.arange(capacity)[None, :] < offset, (block, capacity)),
                jnp.arange(count)[None, :] <= places[:, None],
            ],
            axis=1,
        )
        return attend_rows(query, keys, values, live)

    starts = jnp.arange(count // block, dtype=jnp.int32) * block
    return lax.map(one_block, starts).reshape(count, heads * HD)


def piece_rows(query, keys, values, live):
    count, heads = query.shape[0], query.shape[1]
    own = jnp.arange(heads)[:, None] == jnp.arange(heads)[None, :]
    spread = jnp.where(own[None, :, None, :], query[:, :, :, None], jnp.zeros((), query.dtype))
    spread = spread.reshape(count, heads * HD, heads)
    scores = jnp.einsum("rkf,rfh->rhk", keys, spread, preferred_element_type=jnp.float32) * (
        1.0 / math.sqrt(HD)
    )
    masked = jnp.where(live[:, None, :], scores, NEG)
    highest = jnp.max(masked, axis=2)
    weights = jnp.where(live[:, None, :], jnp.exp(masked - highest[:, :, None]), 0.0)
    total = jnp.sum(weights, axis=2)
    mixed = jnp.einsum(
        "rhk,rkf->rhf", weights.astype(jnp.bfloat16), values, preferred_element_type=jnp.float32
    ).reshape(count, heads, heads, HD)
    summed = jnp.sum(jnp.where(own[None, :, :, None], mixed, 0.0), axis=2)
    return (highest, total, summed)


def piece_batch(query, store, lengths):
    capacity = store.shape[2]
    live = jnp.arange(capacity)[None, :] < lengths[:, None]
    return piece_rows(query, store[:, 0], store[:, 1], live)


def home_partial(query, fresh_key, fresh_value, cache, lengths):
    count, capacity = (cache.shape[0], cache.shape[2])
    keys = jnp.concatenate([cache[:, 0], fresh_key.reshape(count, 1, -1)], axis=1)
    values = jnp.concatenate([cache[:, 1], fresh_value.reshape(count, 1, -1)], axis=1)
    live = jnp.concatenate(
        [jnp.arange(capacity)[None, :] < lengths[:, None], jnp.ones((count, 1), jnp.bool_)], axis=1
    )
    return piece_rows(query, keys, values, live)


def combine(parts):
    highest = reduce(jnp.maximum, [part[0] for part in parts])
    factors = [jnp.exp(part[0] - highest) for part in parts]
    upper = reduce(jnp.add, [factor[:, :, None] * part[2] for factor, part in zip(factors, parts)])
    lower = reduce(jnp.add, [factor * part[1] for factor, part in zip(factors, parts)])
    return (upper / lower[:, :, None]).astype(jnp.bfloat16)


def local(
    prefill_x,
    decode_x,
    ln_gain,
    ln_bias,
    qkv_weight,
    qkv_bias,
    prior_cache,
    prefill_offset,
    home_cache,
    piece_len,
    side_store,
):
    count = prefill_x.shape[0]
    requests = decode_x.shape[0]
    rows = jnp.concatenate([prefill_x, decode_x], axis=0)
    ring = lax.axis_size("ty")
    y = lax.axis_index("ty")
    z = lax.axis_index("tz")
    up = [(i, (i + 1) % ring) for i in range(ring)]
    down = [(i, (i - 1) % ring) for i in range(ring)]
    half = rows.shape[0] // 2

    def around(block):
        below = lax.ppermute(block, "ty", up)
        above = lax.ppermute(block, "ty", down)
        across = jnp.concatenate(
            [lax.ppermute(below[:half], "ty", up), lax.ppermute(above[half:], "ty", down)], axis=0
        )
        return [block, below, above, across]

    partner = lax.ppermute(rows, "tz", [(0, 1), (1, 0)])
    pieces = around(rows) + around(partner)
    whole = jnp.concatenate(pieces, axis=1)
    spots = jnp.stack([y, (y + ring - 1) % ring, (y + 1) % ring, (y + 2) % ring])
    order = jnp.concatenate([spots * 2 + z, spots * 2 + (1 - z)]).astype(jnp.int32)

    def feature_order(table):
        return table.reshape(order.shape[0], -1)[order].reshape(table.shape)

    gain, shift = feature_order(ln_gain), feature_order(ln_bias)
    weight = jnp.transpose(qkv_weight, (1, 0, 2))
    own_query, new_key, new_value = project(
        whole[count:],
        0,
        requests,
        gain,
        shift,
        weight,
        qkv_bias,
        piece_len[:, 0] + piece_len[:, 1] + piece_len[:, 2],
        order,
    )
    home_parts = home_partial(own_query, new_key, new_value, home_cache, piece_len[:, 1])
    groups = lax.axis_size("group")
    forward = [(i, (i + 1) % groups) for i in range(groups)]
    backward = [((i + 1) % groups, i) for i in range(groups)]
    heads = own_query.shape[1]

    def ask(lengths, pairs):
        packed = jnp.concatenate(
            [own_query.astype(jnp.float32).reshape(requests, -1), lengths[:, None].astype(jnp.float32)],
            axis=1,
        )
        got = lax.ppermute(packed, "group", pairs)
        return got[:, :-1].reshape(own_query.shape).astype(own_query.dtype), got[:, -1].astype(jnp.int32)

    def answer(parts, pairs):
        highest, total, summed = parts
        packed = jnp.concatenate([summed, highest[:, :, None], total[:, :, None]], axis=2)
        got = lax.ppermute(packed, "group", pairs)
        return (got[:, :, HD], got[:, :, HD + 1], got[:, :, :HD])

    prev_query, prev_len = ask(piece_len[:, 2], forward)
    next_query, next_len = ask(piece_len[:, 0], backward)
    right_for_prev = piece_batch(prev_query, side_store[:requests], prev_len)
    left_for_next = piece_batch(next_query, side_store[requests:], next_len)
    query, fresh_key, fresh_value = project(
        whole,
        0,
        count,
        gain,
        shift,
        weight,
        qkv_bias,
        prefill_offset[0] + jnp.arange(count, dtype=jnp.int32),
        order,
    )
    right_for_prev, left_for_next, query, fresh_key, fresh_value = lax.optimization_barrier(
        (right_for_prev, left_for_next, query, fresh_key, fresh_value)
    )
    right_parts = answer(right_for_prev, backward)
    left_parts = answer(left_for_next, forward)
    prefill_out = prefill_attend(query, fresh_key, fresh_value, prior_cache[0], prefill_offset[0])
    decode_out = combine([left_parts, home_parts, right_parts]).reshape(requests, -1)
    return (prefill_out, decode_out)


def solution(mesh):
    devices = mesh.devices.reshape(mesh.devices.shape[0], -1, 2)
    split = jax.sharding.Mesh(devices, ("group", "ty", "tz"))
    tp = ("ty", "tz")
    inner = jax.shard_map(
        local,
        mesh=split,
        in_specs=(
            P("group", tp),
            P("group", tp),
            P(),
            P(),
            P(None, None, tp),
            P(None, tp),
            P("group", None, None, tp),
            P("group"),
            P("group", None, None, tp),
            P("group", None),
            P("group", None, None, tp),
        ),
        out_specs=(P("group", tp), P("group", tp)),
        check_vma=False,
    )
    return inner
```

```python
from functools import reduce
import math

import jax
import jax.numpy as jnp
from jax import lax
from jax.experimental import pallas as pl
from jax.experimental.pallas import tpu as pltpu
from jax.sharding import PartitionSpec as P

HD = 128
ROT = 32


EPS = 1e-05
NEG = -1e30


def with_halo(block, sides, width):
    for axis, dim in sides:
        count = lax.axis_size(axis)
        forward = [(i, i + 1) for i in range(count - 1)]
        forward.append((count - 1, 0))
        backward = [(target, source) for source, target in forward]
        low = lax.ppermute(
            lax.slice_in_dim(block, block.shape[dim] - width, None, axis=dim), axis, forward
        )
        high = lax.ppermute(lax.slice_in_dim(block, 0, width, axis=dim), axis, backward)
        block = jnp.concatenate([low, block, high], axis=dim)
    return block


def layer_norm(rows, gain, shift):
    rows = rows.astype(jnp.float32)
    middle = jnp.mean(rows, axis=-1, keepdims=True)
    centred = rows - middle
    spread = jnp.mean(centred * centred, axis=-1, keepdims=True)
    return (centred * lax.rsqrt(spread + EPS) * gain + shift).astype(jnp.bfloat16)


def rotate(vectors, positions):
    half = ROT // 2
    steps = jnp.arange(half, dtype=jnp.float32) * (2.0 / ROT)
    frequency = jnp.exp(-math.log(10000.0) * steps)
    angle = positions.astype(jnp.float32)[:, None] * frequency[None, :]
    cosine = jnp.cos(angle)[:, None, :]
    sine = jnp.sin(angle)[:, None, :]
    first = vectors[..., :half]
    second = vectors[..., half:ROT]
    return jnp.concatenate(
        [first * cosine - second * sine, second * cosine + first * sine, vectors[..., ROT:]],
        axis=-1,
    )


def qkv_kernel(order_ref, x_ref, gain_ref, shift_ref, w_ref, o_ref):
    rows = x_ref[...].astype(jnp.float32)
    middle = jnp.mean(rows, axis=-1, keepdims=True)
    centred = rows - middle
    spread = jnp.mean(centred * centred, axis=-1, keepdims=True)
    normed = (centred * lax.rsqrt(spread + EPS) * gain_ref[...] + shift_ref[...]).astype(
        jnp.bfloat16
    )
    parts, depth, width = w_ref.shape
    blocks = order_ref.shape[0]
    size = depth // blocks
    for c in range(parts):
        total = jnp.zeros((rows.shape[0], width), jnp.float32)
        for j in range(blocks):
            start = pl.multiple_of(order_ref[j] * size, size)
            total += jnp.dot(
                normed[:, j * size : (j + 1) * size],
                w_ref[c, pl.ds(start, size), :],
                preferred_element_type=jnp.float32,
            )
        o_ref[:, c * width : (c + 1) * width] = total


def qkv_matmul(whole, first, rows, gain, shift, weight, order):
    depth = whole.shape[1]
    parts, _, width = weight.shape
    chunk = 256 if rows % 256 == 0 else rows
    skip = first // chunk
    return pl.pallas_call(
        qkv_kernel,
        out_shape=jax.ShapeDtypeStruct((rows, parts * width), jnp.float32),
        grid_spec=pltpu.PrefetchScalarGridSpec(
            num_scalar_prefetch=1,
            grid=(rows // chunk,),
            in_specs=[
                pl.BlockSpec((chunk, depth), lambda i, order: (i + skip, 0)),
                pl.BlockSpec((1, depth), lambda i, order: (0, 0)),
                pl.BlockSpec((1, depth), lambda i, order: (0, 0)),
                pl.BlockSpec((parts, depth, width), lambda i, order: (0, 0, 0)),
            ],
            out_specs=pl.BlockSpec((chunk, parts * width), lambda i, order: (i, 0)),
        ),
        compiler_params=pltpu.CompilerParams(
            dimension_semantics=("arbitrary",), vmem_limit_bytes=48 * 1024 * 1024
        ),
        cost_estimate=pl.CostEstimate(
            flops=2 * rows * depth * parts * width,
            bytes_accessed=2 * rows * depth + 2 * depth * parts * width + 4 * rows * parts * width,
            transcendentals=rows,
        ),
    )(order, whole, gain.reshape(1, depth), shift.reshape(1, depth), weight)


def project(whole, first, count, gain, shift, weight, bias, positions, order):
    width = weight.shape[2]
    mixed = qkv_matmul(whole, first, count, gain, shift, weight, order)
    mixed = (mixed + bias.reshape(1, 3 * width)).reshape(count, 3, width // HD, HD)
    query = rotate(mixed[:, 0], positions).astype(jnp.bfloat16)
    fresh_key = rotate(mixed[:, 1], positions).astype(jnp.bfloat16)
    fresh_value = mixed[:, 2].astype(jnp.bfloat16)
    return (query, fresh_key, fresh_value)


def attend_rows(query, keys, values, live):
    scores = jnp.einsum("qhd,khd->hqk", query, keys, preferred_element_type=jnp.float32) * (
        1.0 / math.sqrt(HD)
    )
    masked = jnp.where(live[None], scores, NEG)
    highest = jnp.max(masked, axis=2, keepdims=True)
    weights = jnp.where(live[None], jnp.exp(masked - highest), 0.0)
    total = jnp.sum(weights, axis=2)
    mixed = jnp.einsum(
        "hqk,khd->qhd", weights.astype(jnp.bfloat16), values, preferred_element_type=jnp.float32
    )
    return (mixed / jnp.transpose(total)[:, :, None]).astype(jnp.bfloat16)


def prefill_attend(query, fresh_key, fresh_value, prior, offset):
    count, heads = (query.shape[0], query.shape[1])
    capacity = prior.shape[1]
    keys = jnp.concatenate([prior[0].reshape(capacity, heads, HD), fresh_key], axis=0)
    values = jnp.concatenate([prior[1].reshape(capacity, heads, HD), fresh_value], axis=0)
    block = min(count, 512)

    def one_block(start):
        places = start + jnp.arange(block, dtype=jnp.int32)
        live = jnp.concatenate(
            [
                jnp.broadcast_to(jnp.arange(capacity)[None, :] < offset, (block, capacity)),
                jnp.arange(count)[None, :] <= places[:, None],
            ],
            axis=1,
        )
        return attend_rows(query, keys, values, live)

    starts = jnp.arange(count // block, dtype=jnp.int32) * block
    return lax.map(one_block, starts).reshape(count, heads * HD)


def piece_rows(query, keys, values, live):
    count, heads = query.shape[0], query.shape[1]
    own = jnp.arange(heads)[:, None] == jnp.arange(heads)[None, :]
    spread = jnp.where(own[None, :, None, :], query[:, :, :, None], jnp.zeros((), query.dtype))
    spread = spread.reshape(count, heads * HD, heads)
    scores = jnp.einsum("rkf,rfh->rhk", keys, spread, preferred_element_type=jnp.float32) * (
        1.0 / math.sqrt(HD)
    )
    masked = jnp.where(live[:, None, :], scores, NEG)
    highest = jnp.max(masked, axis=2)
    weights = jnp.where(live[:, None, :], jnp.exp(masked - highest[:, :, None]), 0.0)
    total = jnp.sum(weights, axis=2)
    mixed = jnp.einsum(
        "rhk,rkf->rhf", weights.astype(jnp.bfloat16), values, preferred_element_type=jnp.float32
    ).reshape(count, heads, heads, HD)
    summed = jnp.sum(jnp.where(own[None, :, :, None], mixed, 0.0), axis=2)
    return (highest, total, summed)


def piece_batch(query, store, lengths):
    capacity = store.shape[2]
    live = jnp.arange(capacity)[None, :] < lengths[:, None]
    return piece_rows(query, store[:, 0], store[:, 1], live)


def home_partial(query, fresh_key, fresh_value, cache, lengths):
    count, capacity = (cache.shape[0], cache.shape[2])
    keys = jnp.concatenate([cache[:, 0], fresh_key.reshape(count, 1, -1)], axis=1)
    values = jnp.concatenate([cache[:, 1], fresh_value.reshape(count, 1, -1)], axis=1)
    live = jnp.concatenate(
        [jnp.arange(capacity)[None, :] < lengths[:, None], jnp.ones((count, 1), jnp.bool_)], axis=1
    )
    return piece_rows(query, keys, values, live)


def combine(parts):
    highest = reduce(jnp.maximum, [part[0] for part in parts])
    factors = [jnp.exp(part[0] - highest) for part in parts]
    upper = reduce(jnp.add, [factor[:, :, None] * part[2] for factor, part in zip(factors, parts)])
    lower = reduce(jnp.add, [factor * part[1] for factor, part in zip(factors, parts)])
    return (upper / lower[:, :, None]).astype(jnp.bfloat16)


def local(
    prefill_x,
    decode_x,
    ln_gain,
    ln_bias,
    qkv_weight,
    qkv_bias,
    prior_cache,
    prefill_offset,
    home_cache,
    piece_len,
    side_store,
):
    count = prefill_x.shape[0]
    requests = decode_x.shape[0]
    rows = jnp.concatenate([prefill_x, decode_x], axis=0)
    ring = lax.axis_size("ty")
    y = lax.axis_index("ty")
    z = lax.axis_index("tz")
    up = [(i, (i + 1) % ring) for i in range(ring)]
    down = [(i, (i - 1) % ring) for i in range(ring)]
    half = rows.shape[0] // 2

    def around(block):
        below = lax.ppermute(block, "ty", up)
        above = lax.ppermute(block, "ty", down)
        across = jnp.concatenate(
            [lax.ppermute(below[:half], "ty", up), lax.ppermute(above[half:], "ty", down)], axis=0
        )
        return [block, below, above, across]

    partner = lax.ppermute(rows, "tz", [(0, 1), (1, 0)])
    pieces = around(rows) + around(partner)
    whole = jnp.concatenate(pieces, axis=1)
    spots = jnp.stack([y, (y + ring - 1) % ring, (y + 1) % ring, (y + 2) % ring])
    order = jnp.concatenate([spots * 2 + z, spots * 2 + (1 - z)]).astype(jnp.int32)

    def feature_order(table):
        return table.reshape(order.shape[0], -1)[order].reshape(table.shape)

    gain, shift = feature_order(ln_gain), feature_order(ln_bias)
    weight = jnp.transpose(qkv_weight, (1, 0, 2))
    own_query, new_key, new_value = project(
        whole[count:],
        0,
        requests,
        gain,
        shift,
        weight,
        qkv_bias,
        piece_len[:, 0] + piece_len[:, 1] + piece_len[:, 2],
        order,
    )
    home_parts = home_partial(own_query, new_key, new_value, home_cache, piece_len[:, 1])
    groups = lax.axis_size("group")
    forward = [(i, (i + 1) % groups) for i in range(groups)]
    backward = [((i + 1) % groups, i) for i in range(groups)]
    heads = own_query.shape[1]

    def ask(lengths, pairs):
        packed = jnp.concatenate(
            [own_query.astype(jnp.float32).reshape(requests, -1), lengths[:, None].astype(jnp.float32)],
            axis=1,
        )
        got = lax.ppermute(packed, "group", pairs)
        return got[:, :-1].reshape(own_query.shape).astype(own_query.dtype), got[:, -1].astype(jnp.int32)

    def answer(parts, pairs):
        highest, total, summed = parts
        packed = jnp.concatenate([summed, highest[:, :, None], total[:, :, None]], axis=2)
        got = lax.ppermute(packed, "group", pairs)
        return (got[:, :, HD], got[:, :, HD + 1], got[:, :, :HD])

    prev_query, prev_len = ask(piece_len[:, 2], forward)
    next_query, next_len = ask(piece_len[:, 0], backward)
    right_parts = answer(piece_batch(prev_query, side_store[:requests], prev_len), backward)
    left_parts = answer(piece_batch(next_query, side_store[requests:], next_len), forward)
    query, fresh_key, fresh_value = project(
        whole,
        0,
        count,
        gain,
        shift,
        weight,
        qkv_bias,
        prefill_offset[0] + jnp.arange(count, dtype=jnp.int32),
        order,
    )
    prefill_out = prefill_attend(query, fresh_key, fresh_value, prior_cache[0], prefill_offset[0])
    decode_out = combine([left_parts, home_parts, right_parts]).reshape(requests, -1)
    return (prefill_out, decode_out)


def solution(mesh):
    devices = mesh.devices.reshape(mesh.devices.shape[0], -1, 2)
    split = jax.sharding.Mesh(devices, ("group", "ty", "tz"))
    tp = ("ty", "tz")
    inner = jax.shard_map(
        local,
        mesh=split,
        in_specs=(
            P("group", tp),
            P("group", tp),
            P(),
            P(),
            P(None, None, tp),
            P(None, tp),
            P("group", None, None, tp),
            P("group"),
            P("group", None, None, tp),
            P("group", None),
            P("group", None, None, tp),
        ),
        out_specs=(P("group", tp), P("group", tp)),
        check_vma=False,
    )
    return inner
```

```python
from functools import reduce
import math

import jax
import jax.numpy as jnp
from jax import lax
from jax.experimental import pallas as pl
from jax.experimental.pallas import tpu as pltpu
from jax.sharding import PartitionSpec as P

HD = 128
ROT = 32


EPS = 1e-05
NEG = -1e30


def with_halo(block, sides, width):
    for axis, dim in sides:
        count = lax.axis_size(axis)
        forward = [(i, i + 1) for i in range(count - 1)]
        forward.append((count - 1, 0))
        backward = [(target, source) for source, target in forward]
        low = lax.ppermute(
            lax.slice_in_dim(block, block.shape[dim] - width, None, axis=dim), axis, forward
        )
        high = lax.ppermute(lax.slice_in_dim(block, 0, width, axis=dim), axis, backward)
        block = jnp.concatenate([low, block, high], axis=dim)
    return block


def layer_norm(rows, gain, shift):
    rows = rows.astype(jnp.float32)
    middle = jnp.mean(rows, axis=-1, keepdims=True)
    centred = rows - middle
    spread = jnp.mean(centred * centred, axis=-1, keepdims=True)
    return (centred * lax.rsqrt(spread + EPS) * gain + shift).astype(jnp.bfloat16)


def rotate(vectors, positions):
    half = ROT // 2
    steps = jnp.arange(half, dtype=jnp.float32) * (2.0 / ROT)
    frequency = jnp.exp(-math.log(10000.0) * steps)
    angle = positions.astype(jnp.float32)[:, None] * frequency[None, :]
    cosine = jnp.cos(angle)[:, None, :]
    sine = jnp.sin(angle)[:, None, :]
    first = vectors[..., :half]
    second = vectors[..., half:ROT]
    return jnp.concatenate(
        [first * cosine - second * sine, second * cosine + first * sine, vectors[..., ROT:]],
        axis=-1,
    )


def qkv_kernel(order_ref, x_ref, gain_ref, shift_ref, w_ref, o_ref):
    rows = x_ref[...].astype(jnp.float32)
    middle = jnp.mean(rows, axis=-1, keepdims=True)
    centred = rows - middle
    spread = jnp.mean(centred * centred, axis=-1, keepdims=True)
    normed = (centred * lax.rsqrt(spread + EPS) * gain_ref[...] + shift_ref[...]).astype(
        jnp.bfloat16
    )
    parts, depth, width = w_ref.shape
    blocks = order_ref.shape[0]
    size = depth // blocks
    for c in range(parts):
        total = jnp.zeros((rows.shape[0], width), jnp.float32)
        for j in range(blocks):
            start = pl.multiple_of(order_ref[j] * size, size)
            total += jnp.dot(
                normed[:, j * size : (j + 1) * size],
                w_ref[c, pl.ds(start, size), :],
                preferred_element_type=jnp.float32,
            )
        o_ref[:, c * width : (c + 1) * width] = total


def qkv_matmul(whole, first, rows, gain, shift, weight, order):
    depth = whole.shape[1]
    parts, _, width = weight.shape
    chunk = 128 if rows % 128 == 0 else rows
    skip = first // chunk
    return pl.pallas_call(
        qkv_kernel,
        out_shape=jax.ShapeDtypeStruct((rows, parts * width), jnp.float32),
        grid_spec=pltpu.PrefetchScalarGridSpec(
            num_scalar_prefetch=1,
            grid=(rows // chunk,),
            in_specs=[
                pl.BlockSpec((chunk, depth), lambda i, order: (i + skip, 0)),
                pl.BlockSpec((1, depth), lambda i, order: (0, 0)),
                pl.BlockSpec((1, depth), lambda i, order: (0, 0)),
                pl.BlockSpec((parts, depth, width), lambda i, order: (0, 0, 0)),
            ],
            out_specs=pl.BlockSpec((chunk, parts * width), lambda i, order: (i, 0)),
        ),
        compiler_params=pltpu.CompilerParams(
            dimension_semantics=("arbitrary",), vmem_limit_bytes=48 * 1024 * 1024
        ),
        cost_estimate=pl.CostEstimate(
            flops=2 * rows * depth * parts * width,
            bytes_accessed=2 * rows * depth + 2 * depth * parts * width + 4 * rows * parts * width,
            transcendentals=rows,
        ),
    )(order, whole, gain.reshape(1, depth), shift.reshape(1, depth), weight)


def project(whole, first, count, gain, shift, weight, bias, positions, order):
    width = weight.shape[2]
    mixed = qkv_matmul(whole, first, count, gain, shift, weight, order)
    mixed = (mixed + bias.reshape(1, 3 * width)).reshape(count, 3, width // HD, HD)
    query = rotate(mixed[:, 0], positions).astype(jnp.bfloat16)
    fresh_key = rotate(mixed[:, 1], positions).astype(jnp.bfloat16)
    fresh_value = mixed[:, 2].astype(jnp.bfloat16)
    return (query, fresh_key, fresh_value)


def attend_rows(query, keys, values, live):
    outs = []
    for h in range(query.shape[1]):
        scores = lax.dot_general(
            query[:, h],
            keys[:, h],
            (((1,), (1,)), ((), ())),
            preferred_element_type=jnp.float32,
        ) * (1.0 / math.sqrt(HD))
        masked = jnp.where(live, scores, NEG)
        highest = jnp.max(masked, axis=1, keepdims=True)
        weights = jnp.where(live, jnp.exp(masked - highest), 0.0)
        total = jnp.sum(weights, axis=1, keepdims=True)
        mixed = jnp.dot(
            weights.astype(jnp.bfloat16), values[:, h], preferred_element_type=jnp.float32
        )
        outs.append((mixed / total).astype(jnp.bfloat16))
    return jnp.stack(outs, axis=1)


def prefill_attend(query, fresh_key, fresh_value, prior, offset):
    count, heads = (query.shape[0], query.shape[1])
    capacity = prior.shape[1]
    keys = jnp.concatenate([prior[0].reshape(capacity, heads, HD), fresh_key], axis=0)
    values = jnp.concatenate([prior[1].reshape(capacity, heads, HD), fresh_value], axis=0)
    block = min(count, 512)

    def one_block(start):
        places = start + jnp.arange(block, dtype=jnp.int32)
        live = jnp.concatenate(
            [
                jnp.broadcast_to(jnp.arange(capacity)[None, :] < offset, (block, capacity)),
                jnp.arange(count)[None, :] <= places[:, None],
            ],
            axis=1,
        )
        return attend_rows(query, keys, values, live)

    starts = jnp.arange(count // block, dtype=jnp.int32) * block
    return lax.map(one_block, starts).reshape(count, heads * HD)


def piece_rows(query, keys, values, live):
    count, heads = query.shape[0], query.shape[1]
    own = jnp.arange(heads)[:, None] == jnp.arange(heads)[None, :]
    spread = jnp.where(own[None, :, None, :], query[:, :, :, None], jnp.zeros((), query.dtype))
    spread = spread.reshape(count, heads * HD, heads)
    scores = jnp.einsum("rkf,rfh->rhk", keys, spread, preferred_element_type=jnp.float32) * (
        1.0 / math.sqrt(HD)
    )
    masked = jnp.where(live[:, None, :], scores, NEG)
    highest = jnp.max(masked, axis=2)
    weights = jnp.where(live[:, None, :], jnp.exp(masked - highest[:, :, None]), 0.0)
    total = jnp.sum(weights, axis=2)
    mixed = jnp.einsum(
        "rhk,rkf->rhf", weights.astype(jnp.bfloat16), values, preferred_element_type=jnp.float32
    ).reshape(count, heads, heads, HD)
    summed = jnp.sum(jnp.where(own[None, :, :, None], mixed, 0.0), axis=2)
    return (highest, total, summed)


def piece_batch(query, store, lengths):
    capacity = store.shape[2]
    live = jnp.arange(capacity)[None, :] < lengths[:, None]
    return piece_rows(query, store[:, 0], store[:, 1], live)


def home_partial(query, fresh_key, fresh_value, cache, lengths):
    count, capacity = (cache.shape[0], cache.shape[2])
    keys = jnp.concatenate([cache[:, 0], fresh_key.reshape(count, 1, -1)], axis=1)
    values = jnp.concatenate([cache[:, 1], fresh_value.reshape(count, 1, -1)], axis=1)
    live = jnp.concatenate(
        [jnp.arange(capacity)[None, :] < lengths[:, None], jnp.ones((count, 1), jnp.bool_)], axis=1
    )
    return piece_rows(query, keys, values, live)


def combine(parts):
    highest = reduce(jnp.maximum, [part[0] for part in parts])
    factors = [jnp.exp(part[0] - highest) for part in parts]
    upper = reduce(jnp.add, [factor[:, :, None] * part[2] for factor, part in zip(factors, parts)])
    lower = reduce(jnp.add, [factor * part[1] for factor, part in zip(factors, parts)])
    return (upper / lower[:, :, None]).astype(jnp.bfloat16)


def local(
    prefill_x,
    decode_x,
    ln_gain,
    ln_bias,
    qkv_weight,
    qkv_bias,
    prior_cache,
    prefill_offset,
    home_cache,
    piece_len,
    side_store,
):
    count = prefill_x.shape[0]
    requests = decode_x.shape[0]
    rows = jnp.concatenate([prefill_x, decode_x], axis=0)
    ring = lax.axis_size("ty")
    y = lax.axis_index("ty")
    z = lax.axis_index("tz")
    up = [(i, (i + 1) % ring) for i in range(ring)]
    down = [(i, (i - 1) % ring) for i in range(ring)]
    half = rows.shape[0] // 2

    def around(block):
        below = lax.ppermute(block, "ty", up)
        above = lax.ppermute(block, "ty", down)
        across = jnp.concatenate(
            [lax.ppermute(below[:half], "ty", up), lax.ppermute(above[half:], "ty", down)], axis=0
        )
        return [block, below, above, across]

    partner = lax.ppermute(rows, "tz", [(0, 1), (1, 0)])
    pieces = around(rows) + around(partner)
    whole = jnp.concatenate(pieces, axis=1)
    spots = jnp.stack([y, (y + ring - 1) % ring, (y + 1) % ring, (y + 2) % ring])
    order = jnp.concatenate([spots * 2 + z, spots * 2 + (1 - z)]).astype(jnp.int32)

    def feature_order(table):
        return table.reshape(order.shape[0], -1)[order].reshape(table.shape)

    gain, shift = feature_order(ln_gain), feature_order(ln_bias)
    weight = jnp.transpose(qkv_weight, (1, 0, 2))
    own_query, new_key, new_value = project(
        whole[count:],
        0,
        requests,
        gain,
        shift,
        weight,
        qkv_bias,
        piece_len[:, 0] + piece_len[:, 1] + piece_len[:, 2],
        order,
    )
    home_parts = home_partial(own_query, new_key, new_value, home_cache, piece_len[:, 1])
    groups = lax.axis_size("group")
    forward = [(i, (i + 1) % groups) for i in range(groups)]
    backward = [((i + 1) % groups, i) for i in range(groups)]
    heads = own_query.shape[1]

    def ask(lengths, pairs):
        packed = jnp.concatenate(
            [own_query.astype(jnp.float32).reshape(requests, -1), lengths[:, None].astype(jnp.float32)],
            axis=1,
        )
        got = lax.ppermute(packed, "group", pairs)
        return got[:, :-1].reshape(own_query.shape).astype(own_query.dtype), got[:, -1].astype(jnp.int32)

    def answer(parts, pairs):
        highest, total, summed = parts
        packed = jnp.concatenate([summed, highest[:, :, None], total[:, :, None]], axis=2)
        got = lax.ppermute(packed, "group", pairs)
        return (got[:, :, HD], got[:, :, HD + 1], got[:, :, :HD])

    prev_query, prev_len = ask(piece_len[:, 2], forward)
    next_query, next_len = ask(piece_len[:, 0], backward)
    right_parts = answer(piece_batch(prev_query, side_store[:requests], prev_len), backward)
    left_parts = answer(piece_batch(next_query, side_store[requests:], next_len), forward)
    query, fresh_key, fresh_value = project(
        whole,
        0,
        count,
        gain,
        shift,
        weight,
        qkv_bias,
        prefill_offset[0] + jnp.arange(count, dtype=jnp.int32),
        order,
    )
    prefill_out = prefill_attend(query, fresh_key, fresh_value, prior_cache[0], prefill_offset[0])
    decode_out = combine([left_parts, home_parts, right_parts]).reshape(requests, -1)
    return (prefill_out, decode_out)


def solution(mesh):
    devices = mesh.devices.reshape(mesh.devices.shape[0], -1, 2)
    split = jax.sharding.Mesh(devices, ("group", "ty", "tz"))
    tp = ("ty", "tz")
    inner = jax.shard_map(
        local,
        mesh=split,
        in_specs=(
            P("group", tp),
            P("group", tp),
            P(),
            P(),
            P(None, None, tp),
            P(None, tp),
            P("group", None, None, tp),
            P("group"),
            P("group", None, None, tp),
            P("group", None),
            P("group", None, None, tp),
        ),
        out_specs=(P("group", tp), P("group", tp)),
        check_vma=False,
    )
    return inner
```

```python
from functools import reduce
import math

import jax
import jax.numpy as jnp
from jax import lax
from jax.experimental import pallas as pl
from jax.experimental.pallas import tpu as pltpu
from jax.sharding import PartitionSpec as P

HD = 128
ROT = 32


EPS = 1e-05
NEG = -1e30


def with_halo(block, sides, width):
    for axis, dim in sides:
        count = lax.axis_size(axis)
        forward = [(i, i + 1) for i in range(count - 1)]
        forward.append((count - 1, 0))
        backward = [(target, source) for source, target in forward]
        low = lax.ppermute(
            lax.slice_in_dim(block, block.shape[dim] - width, None, axis=dim), axis, forward
        )
        high = lax.ppermute(lax.slice_in_dim(block, 0, width, axis=dim), axis, backward)
        block = jnp.concatenate([low, block, high], axis=dim)
    return block


def layer_norm(rows, gain, shift):
    rows = rows.astype(jnp.float32)
    middle = jnp.mean(rows, axis=-1, keepdims=True)
    centred = rows - middle
    spread = jnp.mean(centred * centred, axis=-1, keepdims=True)
    return (centred * lax.rsqrt(spread + EPS) * gain + shift).astype(jnp.bfloat16)


def rotate(vectors, positions):
    half = ROT // 2
    steps = jnp.arange(half, dtype=jnp.float32) * (2.0 / ROT)
    frequency = jnp.exp(-math.log(10000.0) * steps)
    angle = positions.astype(jnp.float32)[:, None] * frequency[None, :]
    cosine = jnp.cos(angle)[:, None, :]
    sine = jnp.sin(angle)[:, None, :]
    first = vectors[..., :half]
    second = vectors[..., half:ROT]
    return jnp.concatenate(
        [first * cosine - second * sine, second * cosine + first * sine, vectors[..., ROT:]],
        axis=-1,
    )


def qkv_kernel(order_ref, x_ref, gain_ref, shift_ref, w_ref, o_ref):
    rows = x_ref[...].astype(jnp.float32)
    middle = jnp.mean(rows, axis=-1, keepdims=True)
    centred = rows - middle
    spread = jnp.mean(centred * centred, axis=-1, keepdims=True)
    normed = (centred * lax.rsqrt(spread + EPS) * gain_ref[...] + shift_ref[...]).astype(
        jnp.bfloat16
    )
    parts, depth, width = w_ref.shape
    blocks = order_ref.shape[0]
    size = depth // blocks
    for c in range(parts):
        total = jnp.zeros((rows.shape[0], width), jnp.float32)
        for j in range(blocks):
            start = pl.multiple_of(order_ref[j] * size, size)
            total += jnp.dot(
                normed[:, j * size : (j + 1) * size],
                w_ref[c, pl.ds(start, size), :],
                preferred_element_type=jnp.float32,
            )
        o_ref[:, c * width : (c + 1) * width] = total


def qkv_matmul(whole, first, rows, gain, shift, weight, order):
    depth = whole.shape[1]
    parts, _, width = weight.shape
    chunk = 128 if rows % 128 == 0 else rows
    skip = first // chunk
    return pl.pallas_call(
        qkv_kernel,
        out_shape=jax.ShapeDtypeStruct((rows, parts * width), jnp.float32),
        grid_spec=pltpu.PrefetchScalarGridSpec(
            num_scalar_prefetch=1,
            grid=(rows // chunk,),
            in_specs=[
                pl.BlockSpec((chunk, depth), lambda i, order: (i + skip, 0)),
                pl.BlockSpec((1, depth), lambda i, order: (0, 0)),
                pl.BlockSpec((1, depth), lambda i, order: (0, 0)),
                pl.BlockSpec((parts, depth, width), lambda i, order: (0, 0, 0)),
            ],
            out_specs=pl.BlockSpec((chunk, parts * width), lambda i, order: (i, 0)),
        ),
        compiler_params=pltpu.CompilerParams(
            dimension_semantics=("arbitrary",), vmem_limit_bytes=48 * 1024 * 1024
        ),
        cost_estimate=pl.CostEstimate(
            flops=2 * rows * depth * parts * width,
            bytes_accessed=2 * rows * depth + 2 * depth * parts * width + 4 * rows * parts * width,
            transcendentals=rows,
        ),
    )(order, whole, gain.reshape(1, depth), shift.reshape(1, depth), weight)


def project(whole, first, count, gain, shift, weight, bias, positions, order):
    width = weight.shape[2]
    mixed = qkv_matmul(whole, first, count, gain, shift, weight, order)
    mixed = (mixed + bias.reshape(1, 3 * width)).reshape(count, 3, width // HD, HD)
    query = rotate(mixed[:, 0], positions).astype(jnp.bfloat16)
    fresh_key = rotate(mixed[:, 1], positions).astype(jnp.bfloat16)
    fresh_value = mixed[:, 2].astype(jnp.bfloat16)
    return (query, fresh_key, fresh_value)


def attend_rows(query, keys, values, live):
    scores = jnp.einsum("qhd,khd->hqk", query, keys, preferred_element_type=jnp.float32) * (
        1.0 / math.sqrt(HD)
    )
    masked = jnp.where(live[None], scores, NEG)
    highest = jnp.max(masked, axis=2, keepdims=True)
    weights = jnp.where(live[None], jnp.exp(masked - highest), 0.0)
    total = jnp.sum(weights, axis=2)
    mixed = jnp.einsum(
        "hqk,khd->qhd", weights.astype(jnp.bfloat16), values, preferred_element_type=jnp.float32
    )
    return (mixed / jnp.transpose(total)[:, :, None]).astype(jnp.bfloat16)


def prefill_attend(query, fresh_key, fresh_value, prior, offset):
    count, heads = (query.shape[0], query.shape[1])
    capacity = prior.shape[1]
    keys = jnp.concatenate([prior[0].reshape(capacity, heads, HD), fresh_key], axis=0)
    values = jnp.concatenate([prior[1].reshape(capacity, heads, HD), fresh_value], axis=0)
    block = min(count, 512)

    def one_block(start):
        places = start + jnp.arange(block, dtype=jnp.int32)
        live = jnp.concatenate(
            [
                jnp.broadcast_to(jnp.arange(capacity)[None, :] < offset, (block, capacity)),
                jnp.arange(count)[None, :] <= places[:, None],
            ],
            axis=1,
        )
        return attend_rows(query, keys, values, live)

    starts = jnp.arange(count // block, dtype=jnp.int32) * block
    return lax.map(one_block, starts).reshape(count, heads * HD)


def piece_rows(query, keys, values, live):
    count, heads = query.shape[0], query.shape[1]
    own = jnp.arange(heads)[:, None] == jnp.arange(heads)[None, :]
    spread = jnp.where(own[None, :, None, :], query[:, :, :, None], jnp.zeros((), query.dtype))
    spread = spread.reshape(count, heads * HD, heads)
    scores = jnp.einsum("rkf,rfh->rhk", keys, spread, preferred_element_type=jnp.float32) * (
        1.0 / math.sqrt(HD)
    )
    masked = jnp.where(live[:, None, :], scores, NEG)
    highest = jnp.max(masked, axis=2)
    weights = jnp.where(live[:, None, :], jnp.exp(masked - highest[:, :, None]), 0.0)
    total = jnp.sum(weights, axis=2)
    mixed = jnp.einsum(
        "rhk,rkf->rhf", weights.astype(jnp.bfloat16), values, preferred_element_type=jnp.float32
    ).reshape(count, heads, heads, HD)
    summed = jnp.sum(jnp.where(own[None, :, :, None], mixed, 0.0), axis=2)
    return (highest, total, summed)


def piece_batch(query, store, lengths):
    capacity = store.shape[2]
    live = jnp.arange(capacity)[None, :] < lengths[:, None]
    return piece_rows(query, store[:, 0], store[:, 1], live)


def home_partial(query, fresh_key, fresh_value, cache, lengths):
    count, capacity = (cache.shape[0], cache.shape[2])
    keys = jnp.concatenate([cache[:, 0], fresh_key.reshape(count, 1, -1)], axis=1)
    values = jnp.concatenate([cache[:, 1], fresh_value.reshape(count, 1, -1)], axis=1)
    live = jnp.concatenate(
        [jnp.arange(capacity)[None, :] < lengths[:, None], jnp.ones((count, 1), jnp.bool_)], axis=1
    )
    return piece_rows(query, keys, values, live)


def combine(parts):
    highest = reduce(jnp.maximum, [part[0] for part in parts])
    factors = [jnp.exp(part[0] - highest) for part in parts]
    upper = reduce(jnp.add, [factor[:, :, None] * part[2] for factor, part in zip(factors, parts)])
    lower = reduce(jnp.add, [factor * part[1] for factor, part in zip(factors, parts)])
    return (upper / lower[:, :, None]).astype(jnp.bfloat16)


def local(
    prefill_x,
    decode_x,
    ln_gain,
    ln_bias,
    qkv_weight,
    qkv_bias,
    prior_cache,
    prefill_offset,
    home_cache,
    piece_len,
    side_store,
):
    count = prefill_x.shape[0]
    requests = decode_x.shape[0]
    rows = jnp.concatenate([prefill_x, decode_x], axis=0)
    ring = lax.axis_size("ty")
    y = lax.axis_index("ty")
    z = lax.axis_index("tz")
    up = [(i, (i + 1) % ring) for i in range(ring)]
    down = [(i, (i - 1) % ring) for i in range(ring)]
    half = rows.shape[0] // 2

    def around(block):
        below = lax.ppermute(block, "ty", up)
        above = lax.ppermute(block, "ty", down)
        across = jnp.concatenate(
            [lax.ppermute(below[:half], "ty", up), lax.ppermute(above[half:], "ty", down)], axis=0
        )
        return [block, below, above, across]

    partner = lax.ppermute(rows, "tz", [(0, 1), (1, 0)])
    pieces = around(rows) + around(partner)
    whole = jnp.concatenate(pieces, axis=1)
    spots = jnp.stack([y, (y + ring - 1) % ring, (y + 1) % ring, (y + 2) % ring])
    order = jnp.concatenate([spots * 2 + z, spots * 2 + (1 - z)]).astype(jnp.int32)

    def feature_order(table):
        return table.reshape(order.shape[0], -1)[order].reshape(table.shape)

    gain, shift = feature_order(ln_gain), feature_order(ln_bias)
    weight = jnp.transpose(qkv_weight, (1, 0, 2))
    own_query, new_key, new_value = project(
        whole[count:],
        0,
        requests,
        gain,
        shift,
        weight,
        qkv_bias,
        piece_len[:, 0] + piece_len[:, 1] + piece_len[:, 2],
        order,
    )
    home_parts = home_partial(own_query, new_key, new_value, home_cache, piece_len[:, 1])
    groups = lax.axis_size("group")
    forward = [(i, (i + 1) % groups) for i in range(groups)]
    backward = [((i + 1) % groups, i) for i in range(groups)]
    heads = own_query.shape[1]

    def ask(lengths, pairs):
        packed = jnp.concatenate(
            [own_query.astype(jnp.float32).reshape(requests, -1), lengths[:, None].astype(jnp.float32)],
            axis=1,
        )
        got = lax.ppermute(packed, "group", pairs)
        return got[:, :-1].reshape(own_query.shape).astype(own_query.dtype), got[:, -1].astype(jnp.int32)

    def answer(parts, pairs):
        highest, total, summed = parts
        packed = jnp.concatenate([summed, highest[:, :, None], total[:, :, None]], axis=2)
        got = lax.ppermute(packed, "group", pairs)
        return (got[:, :, HD], got[:, :, HD + 1], got[:, :, :HD])

    prev_query, prev_len = ask(piece_len[:, 2], forward)
    next_query, next_len = ask(piece_len[:, 0], backward)
    prefill_rows, prev_query, prev_len, next_query, next_len = lax.optimization_barrier(
        (whole, prev_query, prev_len, next_query, next_len)
    )
    right_parts = answer(piece_batch(prev_query, side_store[:requests], prev_len), backward)
    left_parts = answer(piece_batch(next_query, side_store[requests:], next_len), forward)
    query, fresh_key, fresh_value = project(
        prefill_rows,
        0,
        count,
        gain,
        shift,
        weight,
        qkv_bias,
        prefill_offset[0] + jnp.arange(count, dtype=jnp.int32),
        order,
    )
    prefill_out = prefill_attend(query, fresh_key, fresh_value, prior_cache[0], prefill_offset[0])
    decode_out = combine([left_parts, home_parts, right_parts]).reshape(requests, -1)
    return (prefill_out, decode_out)


def solution(mesh):
    devices = mesh.devices.reshape(mesh.devices.shape[0], -1, 2)
    split = jax.sharding.Mesh(devices, ("group", "ty", "tz"))
    tp = ("ty", "tz")
    inner = jax.shard_map(
        local,
        mesh=split,
        in_specs=(
            P("group", tp),
            P("group", tp),
            P(),
            P(),
            P(None, None, tp),
            P(None, tp),
            P("group", None, None, tp),
            P("group"),
            P("group", None, None, tp),
            P("group", None),
            P("group", None, None, tp),
        ),
        out_specs=(P("group", tp), P("group", tp)),
        check_vma=False,
    )
    return inner
```
